128 devices in a mesh: elem: 16 (over x, z), sub: 8 (over y, core).
Axes of the slice: x: 4, y: 4, z: 4, core: 2. Of those that a mesh axis runs over, the one named last changes fastest.
Arguments:
- load_vector: float32 [125, 147456], P(None, ('elem', 'sub')), may hold values from -6 to 6
- fine_scale: float32 [147456], P(('elem', 'sub')), may hold values from 0.3 to 3
- coarse_scale: float32 [32768], P(('elem', 'sub')), may hold values from 0.3 to 3
- parent_owner: int32 [147456], P(('elem', 'sub')), may hold values from 0 to 127, as said below
- parent_pos: int32 [147456], P(('elem', 'sub')), may hold values from 0 to 17, as said below
- child_code: int32 [147456], P(('elem', 'sub')), may hold values from 0 to 8, as said below
- arrival_slot: int32 [294912], P(('elem', 'sub')), may hold values from 0 to 256, as said below
- fine_local: int32 [884736], P(('elem', 'sub')), may hold values from -1 to 6911, as said below
- fine_left: int32 [36864], P(('elem', 'sub')), may hold values from 0 to 6911, as said below
- fine_right: int32 [36864], P(('elem', 'sub')), may hold values from 0 to 6911, as said below
- coarse_local: int32 [196608], P(('elem', 'sub')), may hold values from -1 to 1535, as said below
- coarse_left: int32 [8192], P(('elem', 'sub')), may hold values from 0 to 1535, as said below
- coarse_right: int32 [8192], P(('elem', 'sub')), may hold values from 0 to 1535, as said below
Outputs:
- solution: float32 [125, 147456], P(None, ('elem', 'sub'))
- residual: float32 [125, 147456], P(None, ('elem', 'sub'))
The draws below stay inside these ranges and needn't reach their ends.
Inputs may be any that keep to these rules, and one draw needn't show every extreme that they name: `parent_owner`: each device sends at most 18 fine elements to one owner; some pair of devices reaches 18. `parent_pos`: the fine elements that one device sends to one owner hold distinct slots 0, 1, and so on. `child_code`: 0 to 7: the octant of a refined parent that the element fills; 8: the element equals its unrefined parent. Every coarse element has eight children with codes 0 to 7 or one with code 8. `arrival_slot`: entry j * 18 + k on device o is the local coarse element that receives slot k of device j's message, or 256 where device j sends fewer than k + 1 elements to o; it matches the fine element of device j with parent_owner o and parent_pos k. `fine_local`: local face ids; the pairing is symmetric; faces in the left or right list or on the boundary have -1. `fine_left`: local face ids, distinct, disjoint from the right list; entry k on a device meets entry k of fine_right on the previous device. `fine_right`: local face ids, distinct; entry k on a device meets entry k of fine_left on the next device. `coarse_local`: local face ids; the pairing is symmetric; faces in the left or right list or on the boundary have -1. `coarse_left`: local face ids, distinct, disjoint from the right list; entry k on a device meets entry k of coarse_right on the previous device. `coarse_right`: local face ids, distinct; entry k on a device meets entry k of coarse_left on the next device.
All inputs are finite; a program needn't handle non-finite values.
Results may differ from the reference program's by a relative error of at most 0.0003.
Values sent between devices are 32-bit elements; how exact they have to be, the bound alone decides.
No kernel may reach another device: no remote copies, remote signals or barrier semaphores. Data moves between devices by JAX's collectives and lax.ppermute only.
A program may use at most 64 MiB of HBM per device.

```python
import math
from functools import partial
import jax
import jax.numpy as jnp
import numpy as np
from jax import lax

NODES = 125
EC = 256
ECR = 128
RANKS = 128
EF = 1152
CAP = 18
NSF = 288
NBF = 72
NSC = 64
NBC = 16
NF = 147456
NC = 32768


def shuffle_row(sub_key):
    return jax.random.permutation(sub_key, EF).astype(jnp.int32)


def coarse_side(sub_key):
    flag_key, list_key = jax.random.split(sub_key)
    refined = jnp.zeros((EC,), jnp.int32).at[jax.random.permutation(flag_key, EC)[:ECR]].set(1)
    children = 1 + 7 * refined
    child_end = jnp.cumsum(children).astype(jnp.int32)
    canonical = jnp.arange(EF, dtype=jnp.int32)
    owner_slot = jnp.searchsorted(child_end, canonical, side='right').astype(jnp.int32)
    child_codes = jnp.where(refined[owner_slot] == 1, canonical - (child_end - children)[owner_slot], 8).astype(jnp.int32)
    mixing = jax.random.permutation(list_key, EF)
    return (owner_slot[mixing], child_codes[mixing])


def transfer_layout(key):
    base_key = jax.random.fold_in(key, 101)
    key_list = jax.random.split(base_key, 4)
    mean_count = EF // RANKS
    half_count = RANKS // 2
    drawn_order = jax.random.permutation(key_list[0], RANKS).astype(jnp.int32)
    order_keys = 4 * jnp.argsort(drawn_order).astype(jnp.int32)
    order_keys = order_keys.at[RANKS - 1].set(-8).at[1].set(-4)
    shift_order = jnp.argsort(order_keys, stable=True).astype(jnp.int32)
    surplus = jax.random.randint(key_list[1], (half_count,), 0, mean_count + 1).astype(jnp.int32)
    surplus = surplus.at[0].set(mean_count)
    amounts = jnp.zeros((RANKS,), jnp.int32).at[shift_order[:half_count]].set(mean_count + surplus)
    amounts = amounts.at[shift_order[half_count:]].set(mean_count - surplus)
    seg_ends = jnp.cumsum(amounts).astype(jnp.int32)
    starts = seg_ends - amounts
    places = jnp.arange(EF, dtype=jnp.int32)
    shift_of = jnp.searchsorted(seg_ends, places, side='right').astype(jnp.int32)
    within = places - starts[shift_of]
    rank_ids = jnp.arange(RANKS, dtype=jnp.int32)
    slots, codes = jax.vmap(coarse_side)(jax.random.split(key_list[2], RANKS))
    owner_rank = (rank_ids[:, None] + shift_of[None, :]) % RANKS
    fine_codes = codes[owner_rank, places[None, :]]
    mixes = jax.vmap(shuffle_row)(jax.random.split(key_list[3], RANKS))
    row_ids = jnp.broadcast_to(rank_ids[:, None], (RANKS, EF))
    owners = jnp.zeros((RANKS, EF), jnp.int32).at[row_ids, mixes].set(owner_rank)
    slot_pos = jnp.zeros((RANKS, EF), jnp.int32).at[row_ids, mixes].set(jnp.broadcast_to(within[None, :], (RANKS, EF)))
    child_map = jnp.zeros((RANKS, EF), jnp.int32).at[row_ids, mixes].set(fine_codes)
    from_rank = (rank_ids[:, None] - shift_of[None, :]) % RANKS
    slot_map = jnp.full((RANKS, RANKS * CAP), EC, jnp.int32).at[row_ids, from_rank * CAP + within[None, :]].set(slots)
    return (owners.reshape(-1), slot_pos.reshape(-1), child_map.reshape(-1), slot_map.reshape(-1))


def face_layout(key, salt, elem_count, shared, bare_count):
    key_list = jax.random.split(jax.random.fold_in(key, salt), RANKS)

    def one_device(sub_key):
        face_order = jax.random.permutation(sub_key, 6 * elem_count).astype(jnp.int32)
        right_ids = face_order[:shared]
        left_ids = face_order[shared:2 * shared]
        remaining = face_order[2 * shared + bare_count:]
        first_ids = remaining[0::2]
        second_ids = remaining[1::2]
        local_ids = jnp.full((6 * elem_count,), -1, jnp.int32).at[first_ids].set(second_ids).at[second_ids].set(first_ids)
        return (local_ids, left_ids, right_ids)
    local_ids, left_ids, right_ids = jax.vmap(one_device)(key_list)
    return (local_ids.reshape(-1), left_ids.reshape(-1), right_ids.reshape(-1))


def draw_parent_owner(key, part):
    return transfer_layout(key)[0]


def draw_parent_pos(key, part):
    return transfer_layout(key)[1]


def draw_child_code(key, part):
    return transfer_layout(key)[2]


def draw_arrival_slot(key, part):
    return transfer_layout(key)[3]


def draw_fine_local(key, part):
    return face_layout(key, 7, EF, NSF, NBF)[0]


def draw_fine_left(key, part):
    return face_layout(key, 7, EF, NSF, NBF)[1]


def draw_fine_right(key, part):
    return face_layout(key, 7, EF, NSF, NBF)[2]


def draw_coarse_local(key, part):
    return face_layout(key, 11, EC, NSC, NBC)[0]


def draw_coarse_left(key, part):
    return face_layout(key, 11, EC, NSC, NBC)[1]


def draw_coarse_right(key, part):
    return face_layout(key, 11, EC, NSC, NBC)[2]


def shard_levels(rng, extent, cuts, least, largest):
    factor_of, own = 1.0, jax.random.fold_in(rng, 6)
    for position, blocks in cuts:
        draws = jnp.exp(jax.random.uniform(jax.random.fold_in(own, position), (blocks,), jnp.float32, least / len(cuts), largest / len(cuts)))
        factor_of = factor_of * jnp.repeat(draws, extent[position] // blocks).reshape([-1 if axis == position else 1 for axis in range(len(extent))])
    return factor_of


def scatter_about(own_key, shape, width, limit, cuts=(), held_as=jnp.bfloat16):
    entries = jax.random.normal(own_key, shape, jnp.float32) * width
    if len(cuts) > 0:
        entries = shard_levels(own_key, shape, cuts, -0.22, 0.18) * entries
    return jnp.clip(entries, min=-limit, max=limit).astype(held_as)


def setup_inputs(seed: int = 0) -> dict:
    streams_of = jax.random.split(jax.random.key(seed), 14)
    return {
        "load_vector": scatter_about(streams_of[0], (NODES, NF), 1.0, 6.0, ((1, 128),), jnp.float32),
        "fine_scale": jnp.clip(jnp.exp(math.log(3.0) - 2.3025851 * jax.random.uniform(streams_of[1], (NF,), jnp.float32) ** shard_levels(streams_of[1], (NF,), ((0, 128),), -0.2, 0.2)), 0.3, 3.0),
        "coarse_scale": jnp.clip(jnp.exp(math.log(3.0) - 2.3025851 * jax.random.uniform(streams_of[2], (NC,), jnp.float32) ** shard_levels(streams_of[2], (NC,), ((0, 128),), -0.2, 0.2)), 0.3, 3.0),
        "parent_owner": draw_parent_owner(jax.random.fold_in(streams_of[13], 71), 0),
        "parent_pos": draw_parent_pos(jax.random.fold_in(streams_of[13], 71), 0),
        "child_code": draw_child_code(jax.random.fold_in(streams_of[13], 71), 0),
        "arrival_slot": draw_arrival_slot(jax.random.fold_in(streams_of[13], 71), 0),
        "fine_local": draw_fine_local(jax.random.fold_in(streams_of[13], 71), 0),
        "fine_left": draw_fine_left(jax.random.fold_in(streams_of[13], 71), 0),
        "fine_right": draw_fine_right(jax.random.fold_in(streams_of[13], 71), 0),
        "coarse_local": draw_coarse_local(jax.random.fold_in(streams_of[13], 71), 0),
        "coarse_left": draw_coarse_left(jax.random.fold_in(streams_of[13], 71), 0),
        "coarse_right": draw_coarse_right(jax.random.fold_in(streams_of[13], 71), 0),
    }


highest = lax.Precision.HIGHEST
penalty_weight = 20.0
lower_share = 0.125

def lagrange_rows(points, gll_points):
    values = np.ones((points.shape[0], 5))
    for column in range(5):
        for other_node in range(5):
            if other_node != column:
                values[:, column] *= (points - gll_points[other_node]) / (gll_points[column] - gll_points[other_node])
    return values

def element_tables():
    root_value = math.sqrt(3.0 / 7.0)
    gll_points = np.array([-1.0, -root_value, 0.0, root_value, 1.0])
    gll_weights = np.array([0.1, 49.0 / 90.0, 32.0 / 45.0, 49.0 / 90.0, 0.1])
    identity_mask = np.arange(5)[:, None] == np.arange(5)[None, :]
    spread = gll_points[:, None] - gll_points[None, :]
    spread = np.where(identity_mask, 1.0, spread)
    factor = np.prod(spread, axis=1)
    derive = factor[:, None] / factor[None, :] / spread
    diag_values = np.sum(1.0 / spread, axis=1) - 1.0
    derive = np.where(identity_mask, diag_values[:, None], derive)
    stiff_line = derive.T @ (gll_weights[:, None] * derive)
    mass_line = np.where(identity_mask, gll_weights[None, :], 0.0)
    stiffness = np.kron(np.kron(stiff_line, mass_line), mass_line) + np.kron(np.kron(mass_line, stiff_line), mass_line) + np.kron(np.kron(mass_line, mass_line), stiff_line)
    extract = np.zeros((150, 125))
    face_weight = np.zeros((6, 25))
    for normal in range(3):
        for side_pick in range(2):
            face_id = 2 * normal + side_pick
            for first_pos in range(5):
                for second_pos in range(5):
                    triple = [first_pos, second_pos]
                    triple.insert(normal, 4 * side_pick)
                    node_id = 25 * triple[0] + 5 * triple[1] + triple[2]
                    extract[25 * face_id + 5 * first_pos + second_pos, node_id] = 1.0
                    face_weight[face_id, 5 * first_pos + second_pos] = gll_weights[first_pos] * gll_weights[second_pos]
    face_diag = extract.T @ face_weight.reshape(150)
    node_range = np.arange(125)
    stiff_diag = stiffness[node_range, node_range].copy()
    upper_bound = max(2.0, float(np.max(np.sum(np.abs(stiffness), axis=1) / stiff_diag)))
    halves = np.stack([lagrange_rows((gll_points - 1.0) / 2.0, gll_points), lagrange_rows((gll_points + 1.0) / 2.0, gll_points)])
    return (stiffness, extract, face_weight, face_diag, stiff_diag, upper_bound, halves)

def device_tables():
    stiffness, extract, face_weight, face_diag, stiff_diag, upper_bound, halves = element_tables()
    return (jnp.asarray(stiffness, jnp.float32), jnp.asarray(extract, jnp.float32), jnp.asarray(face_weight, jnp.float32), jnp.asarray(face_diag, jnp.float32), jnp.asarray(stiff_diag, jnp.float32), upper_bound, jnp.asarray(halves, jnp.float32))

def face_flat(vector, extract):
    faces_all = jnp.dot(extract, vector, precision=highest)
    elem_count = vector.shape[-1]
    return faces_all.reshape(6, 25, elem_count).transpose(1, 0, 2).reshape(25, 6 * elem_count)

def combine_faces(vector, scale_row, face_rows, local_ids, left_ids, right_ids, from_left, from_right, stiffness, extract, face_weight):
    elem_count = vector.shape[-1]
    has_local = local_ids >= 0
    partner = jnp.where(has_local[None, :], face_rows[:, jnp.where(has_local, local_ids, 0)], 0.0)
    partner = partner.at[:, left_ids].add(from_left).at[:, right_ids].add(from_right)
    jump_rows = (face_rows - partner).reshape(25, 6, elem_count) * face_weight.T[:, :, None]
    folded = jump_rows.transpose(1, 0, 2).reshape(150, elem_count)
    interior = scale_row[None, :] * jnp.dot(stiffness, vector, precision=highest)
    return interior + penalty_weight * jnp.dot(extract.T, folded, precision=highest)

def inverse_diagonal(scale_row, stiff_diag, face_diag):
    return 1.0 / (scale_row[None, :] * stiff_diag[:, None] + penalty_weight * face_diag[:, None])

def interpolate(values, code_row, halves):
    cube_form = values.reshape(5, 5, 5, -1)
    result = cube_form
    for form_text, divisor in (('tai,ijke->tajke', 4), ('tbj,ijke->tibke', 2), ('tck,ijke->tijce', 1)):
        both_halves = jnp.einsum(form_text, halves, result, precision=highest)
        bit_pick = code_row // divisor % 2
        result = jnp.where(bit_pick[None, None, None, :] == 1, both_halves[1], both_halves[0])
    result = result.reshape(125, -1)
    return jnp.where(code_row[None, :] == 8, values, result)

def chebyshev(start, residual_now, operator_fn, inverse_diag, upper_bound, keep_last):
    low_end = upper_bound * lower_share
    center = 0.5 * (upper_bound + low_end)
    radius = 0.5 * (upper_bound - low_end)
    sigma_value = center / radius
    rho_value = 1.0 / sigma_value
    solution = start
    update = inverse_diag * residual_now / center
    for turn_index in range(3):
        solution = solution + update
        if turn_index < 2 or keep_last:
            residual_now = residual_now - operator_fn(update)
        if turn_index < 2:
            rho_next = 1.0 / (2.0 * sigma_value - rho_value)
            update = rho_next * rho_value * update + 2.0 * rho_next / radius * inverse_diag * residual_now
            rho_value = rho_next
    return (solution, residual_now)

def take_columns(face_rows, column_ids):
    return face_rows[:, column_ids]

def level_apply(blocks, scale_rows, local_ids, left_ids, right_ids, tables):
    stiffness, extract, face_weight = (tables[0], tables[1], tables[2])
    face_rows = jax.vmap(partial(face_flat, extract=extract))(blocks)
    to_left = jax.vmap(take_columns)(face_rows, left_ids)
    to_right = jax.vmap(take_columns)(face_rows, right_ids)
    empty = jnp.zeros_like(to_left[:1])
    from_left = jnp.concatenate([empty, to_right[:-1]], axis=0)
    from_right = jnp.concatenate([to_left[1:], empty], axis=0)
    finish = partial(combine_faces, stiffness=stiffness, extract=extract, face_weight=face_weight)
    return jax.vmap(finish)(blocks, scale_rows, face_rows, local_ids, left_ids, right_ids, from_left, from_right)

def reference(load_vector, fine_scale, coarse_scale, parent_owner, parent_pos, child_code, arrival_slot, fine_local, fine_left, fine_right, coarse_local, coarse_left, coarse_right):
    tables = device_tables()
    face_diag, stiff_diag, upper_bound, halves = (tables[3], tables[4], tables[5], tables[6])
    halves_back = halves.transpose(0, 2, 1)
    fine_rows = fine_scale.reshape(RANKS, EF)
    coarse_rows = coarse_scale.reshape(RANKS, EC)
    fine_ids = (fine_local.reshape(RANKS, 6 * EF), fine_left.reshape(RANKS, NSF), fine_right.reshape(RANKS, NSF))
    coarse_ids = (coarse_local.reshape(RANKS, 6 * EC), coarse_left.reshape(RANKS, NSC), coarse_right.reshape(RANKS, NSC))

    def fine_apply(blocks):
        return level_apply(blocks, fine_rows, fine_ids[0], fine_ids[1], fine_ids[2], tables)

    def coarse_apply(blocks):
        return level_apply(blocks, coarse_rows, coarse_ids[0], coarse_ids[1], coarse_ids[2], tables)
    diag_fn = partial(inverse_diagonal, stiff_diag=stiff_diag, face_diag=face_diag)
    fine_inverse = jax.vmap(diag_fn)(fine_rows)
    coarse_inverse = jax.vmap(diag_fn)(coarse_rows)
    load_blocks = load_vector.reshape(125, RANKS, EF).transpose(1, 0, 2)
    first_x, first_r = chebyshev(jnp.zeros_like(load_blocks), load_blocks, fine_apply, fine_inverse, upper_bound, True)
    owners = parent_owner.reshape(RANKS, EF)
    positions = parent_pos.reshape(RANKS, EF)
    codes = child_code.reshape(RANKS, EF)
    slot_table = arrival_slot.reshape(RANKS, RANKS * CAP)
    sources = jnp.arange(RANKS, dtype=jnp.int32)[:, None]
    parents = slot_table[owners, sources * CAP + positions]
    target = (owners * EC + parents).reshape(-1).astype(jnp.int32)
    pieces = jax.vmap(partial(interpolate, halves=halves_back))(first_r, codes)
    summed = jax.ops.segment_sum(pieces.transpose(0, 2, 1).reshape(RANKS * EF, 125), target, num_segments=RANKS * EC)
    coarse_rhs = summed.reshape(RANKS, EC, 125).transpose(0, 2, 1)
    coarse_x, unused_r = chebyshev(jnp.zeros_like(coarse_rhs), coarse_rhs, coarse_apply, coarse_inverse, upper_bound, False)
    parent_values = coarse_x.transpose(0, 2, 1).reshape(RANKS * EC, 125)[target]
    parent_blocks = parent_values.reshape(RANKS, EF, 125).transpose(0, 2, 1)
    correction = jax.vmap(partial(interpolate, halves=halves))(parent_blocks, codes)
    second_x = first_x + correction
    second_r = first_r - fine_apply(correction)
    final_x, final_r = chebyshev(second_x, second_r, fine_apply, fine_inverse, upper_bound, True)
    solution = final_x.transpose(1, 0, 2).reshape(125, RANKS * EF)
    residual = final_r.transpose(1, 0, 2).reshape(125, RANKS * EF)
    return (solution, residual)
```

```python
import math

import jax
import jax.numpy as jnp
import numpy as np
from jax import lax
from jax.sharding import PartitionSpec as P

highest = lax.Precision.HIGHEST
penalty_weight = 20.0
lower_share = 0.125
AXES = ("elem", "sub")


def passed_along(block, axis, distance):
    devices = range(lax.axis_size(axis))
    route = [(i - distance, i) for i in devices if i - distance in devices]
    return lax.ppermute(block, axis, route)


def lagrange_rows(points, gll_points):
    values = np.ones((points.shape[0], 5))
    for column in range(5):
        for other_node in range(5):
            if other_node != column:
                values[:, column] *= (points - gll_points[other_node]) / (
                    gll_points[column] - gll_points[other_node]
                )
    return values


def element_tables():
    root_value = math.sqrt(3.0 / 7.0)
    gll_points = np.array([-1.0, -root_value, 0.0, root_value, 1.0])
    gll_weights = np.array([0.1, 49.0 / 90.0, 32.0 / 45.0, 49.0 / 90.0, 0.1])
    identity_mask = np.arange(5)[:, None] == np.arange(5)[None, :]
    spread = gll_points[:, None] - gll_points[None, :]
    spread = np.where(identity_mask, 1.0, spread)
    factor = np.prod(spread, axis=1)
    derive = factor[:, None] / factor[None, :] / spread
    diag_values = np.sum(1.0 / spread, axis=1) - 1.0
    derive = np.where(identity_mask, diag_values[:, None], derive)
    stiff_line = derive.T @ (gll_weights[:, None] * derive)
    mass_line = np.where(identity_mask, gll_weights[None, :], 0.0)
    stiffness = (
        np.kron(np.kron(stiff_line, mass_line), mass_line)
        + np.kron(np.kron(mass_line, stiff_line), mass_line)
        + np.kron(np.kron(mass_line, mass_line), stiff_line)
    )
    extract = np.zeros((150, 125))
    face_weight = np.zeros((6, 25))
    face_nodes = np.zeros((6, 25), np.int64)
    for normal in range(3):
        for side_pick in range(2):
            face_id = 2 * normal + side_pick
            for first_pos in range(5):
                for second_pos in range(5):
                    triple = [first_pos, second_pos]
                    triple.insert(normal, 4 * side_pick)
                    node_id = 25 * triple[0] + 5 * triple[1] + triple[2]
                    extract[25 * face_id + 5 * first_pos + second_pos, node_id] = 1.0
                    face_nodes[face_id, 5 * first_pos + second_pos] = node_id
                    face_weight[face_id, 5 * first_pos + second_pos] = (
                        gll_weights[first_pos] * gll_weights[second_pos]
                    )
    face_diag = extract.T @ face_weight.reshape(150)
    node_range = np.arange(125)
    stiff_diag = stiffness[node_range, node_range].copy()
    upper_bound = max(2.0, float(np.max(np.sum(np.abs(stiffness), axis=1) / stiff_diag)))
    halves = np.stack(
        [
            lagrange_rows((gll_points - 1.0) / 2.0, gll_points),
            lagrange_rows((gll_points + 1.0) / 2.0, gll_points),
        ]
    )
    return (stiffness, extract, face_weight, face_diag, stiff_diag, upper_bound, halves, face_nodes)


def to_bf16_grid(values):
    return lax.reduce_precision(values, exponent_bits=8, mantissa_bits=7)


def split3(values):
    high = to_bf16_grid(values)
    rest = values - high
    middle = to_bf16_grid(rest)
    low = rest - middle
    return tuple(part.astype(jnp.bfloat16) for part in (high, middle, low))


def place(onehot, values):
    rows, lanes = values.shape
    width = -(-lanes // 128) * 128
    parts = [jnp.pad(part, ((0, 0), (0, width - lanes))) for part in split3(values)]
    out = jnp.dot(onehot, jnp.concatenate(parts, axis=1), preferred_element_type=jnp.float32)
    total = (out[:, :width] + out[:, width : 2 * width]) + out[:, 2 * width :]
    return total[:, :lanes]


def chebyshev(start, residual_now, operator_fn, inverse_diag, upper_bound, keep_last):
    low_end = upper_bound * lower_share
    center = 0.5 * (upper_bound + low_end)
    radius = 0.5 * (upper_bound - low_end)
    sigma_value = center / radius
    rho_value = 1.0 / sigma_value
    solution = start
    update = inverse_diag * residual_now / center
    for turn_index in range(3):
        solution = solution + update
        if turn_index < 2 or keep_last:
            residual_now = residual_now - operator_fn(update)
        if turn_index < 2:
            rho_next = 1.0 / (2.0 * sigma_value - rho_value)
            update = (
                rho_next * rho_value * update
                + 2.0 * rho_next / radius * inverse_diag * residual_now
            )
            rho_value = rho_next
    return (solution, residual_now)


def onehot_of(rows_ids, column_ids):
    return (rows_ids[:, None] == column_ids[None, :]).astype(jnp.bfloat16)


def level_plan(local_ids, left_ids, right_ids):
    face_count = local_ids.shape[0]
    has_local = local_ids >= 0
    source = jnp.where(has_local, local_ids, 0)
    send_ids = jnp.concatenate([left_ids, right_ids])
    onehot = onehot_of(jnp.arange(face_count, dtype=jnp.int32), send_ids)
    return has_local, source, send_ids, onehot


def apply_level(vector_t, scale_col, plan, mats):
    has_local, source, send_ids, onehot = plan
    stiffness_t, pick, fold, weight = mats
    elem_count = vector_t.shape[0]
    shared = send_ids.shape[0] // 2
    faces = jnp.concatenate(
        [jnp.dot(vector_t, pick[f], precision=highest) for f in range(6)], axis=0
    )
    sent = faces[send_ids]
    from_left = passed_along(sent[shared:], AXES, 1)
    from_right = passed_along(sent[:shared], AXES, -1)
    partner = jnp.where(has_local[:, None], faces[source], 0.0)
    received = jnp.concatenate([from_left, from_right], axis=0)
    partner = partner + place(onehot, received)
    jump = (faces - partner).reshape(6, elem_count, 128) * weight[:, None, :]
    folded = lax.dot_general(
        jump, fold, (((2,), (1,)), ((0,), (0,))), precision=highest
    ).sum(axis=0)
    interior = scale_col * jnp.dot(vector_t, stiffness_t, precision=highest)
    return interior + folded


def interpolate_t(values_t, code_row, mats):
    mixed = jnp.dot(values_t, mats, precision=highest)
    out = jnp.zeros_like(values_t)
    for q in range(9):
        out = jnp.where(code_row[:, None] == q, mixed[:, 128 * q : 128 * q + 125], out)
    return out


def on_device(
    load_vector,
    fine_scale,
    coarse_scale,
    parent_owner,
    parent_pos,
    child_code,
    arrival_slot,
    fine_local,
    fine_left,
    fine_right,
    coarse_local,
    coarse_left,
    coarse_right,
):
    stiffness, extract, face_weight, face_diag, stiff_diag, upper_bound, halves, face_nodes = (
        element_tables()
    )
    pick = np.zeros((6, 125, 128))
    fold = np.zeros((6, 128, 125))
    weight = np.zeros((6, 128))
    for f in range(6):
        for m in range(25):
            pick[f, face_nodes[f, m], m] = 1.0
            fold[f, m, face_nodes[f, m]] = penalty_weight
            weight[f, m] = face_weight[f, m]
    prolong = np.zeros((125, 9 * 128))
    restrict = np.zeros((125, 9 * 128))
    for q in range(9):
        if q == 8:
            matrix = np.eye(125)
        else:
            matrix = np.kron(np.kron(halves[(q // 4) % 2], halves[(q // 2) % 2]), halves[q % 2])
        prolong[:, 128 * q : 128 * q + 125] = matrix.T
        restrict[:, 128 * q : 128 * q + 125] = matrix
    f32 = lambda a: jnp.asarray(a, jnp.float32)
    mats = (f32(stiffness.T), f32(pick), f32(fold), f32(weight))
    prolong = f32(prolong)
    restrict = f32(restrict)
    face_diag = f32(face_diag)
    stiff_diag = f32(stiff_diag)

    fine_plan = level_plan(fine_local, fine_left, fine_right)
    coarse_plan = level_plan(coarse_local, coarse_left, coarse_right)
    fine_col = fine_scale[:, None]
    coarse_col = coarse_scale[:, None]

    def fine_apply(vector_t):
        return apply_level(vector_t, fine_col, fine_plan, mats)

    def coarse_apply(vector_t):
        return apply_level(vector_t, coarse_col, coarse_plan, mats)

    def inverse_diagonal(scale_col):
        return 1.0 / (scale_col * stiff_diag[None, :] + penalty_weight * face_diag[None, :])

    fine_inverse = inverse_diagonal(fine_col)
    coarse_inverse = inverse_diagonal(coarse_col)
    load_t = load_vector.T
    first_x, first_r = chebyshev(
        jnp.zeros_like(load_t), load_t, fine_apply, fine_inverse, upper_bound, True
    )
    rank_count = lax.axis_size(AXES)
    slot_count = arrival_slot.shape[0]
    capacity = slot_count // rank_count
    coarse_count = coarse_scale.shape[0]
    target = parent_owner * capacity + parent_pos
    slot_ids = jnp.arange(slot_count, dtype=jnp.int32)
    coarse_ids = jnp.arange(coarse_count, dtype=jnp.int32)

    pieces = interpolate_t(first_r, child_code, restrict)
    buffer = place(onehot_of(slot_ids, target), pieces)
    arrived = lax.all_to_all(buffer, AXES, 0, 0, tiled=True)
    coarse_rhs = place(onehot_of(coarse_ids, arrival_slot), arrived)
    coarse_x, unused_r = chebyshev(
        jnp.zeros_like(coarse_rhs), coarse_rhs, coarse_apply, coarse_inverse, upper_bound, False
    )
    filled = place(onehot_of(arrival_slot, coarse_ids), coarse_x)
    returned = lax.all_to_all(filled, AXES, 0, 0, tiled=True)
    correction = interpolate_t(place(onehot_of(target, slot_ids), returned), child_code, prolong)
    second_x = first_x + correction
    second_r = first_r - fine_apply(correction)
    final_x, final_r = chebyshev(second_x, second_r, fine_apply, fine_inverse, upper_bound, True)
    return (final_x.T, final_r.T)


def solution(mesh):
    in_specs = (P(None, AXES),) + (P(AXES),) * 12
    out_specs = (P(None, AXES), P(None, AXES))
    return jax.shard_map(
        on_device, mesh=mesh, in_specs=in_specs, out_specs=out_specs, check_vma=False
    )
```

```python
import math

import jax
import jax.numpy as jnp
import numpy as np
from jax import lax
from jax.sharding import PartitionSpec as P

highest = lax.Precision.HIGHEST
penalty_weight = 20.0
lower_share = 0.125
AXES = ("elem", "sub")


def passed_along(block, axis, distance):
    devices = range(lax.axis_size(axis))
    route = [(i - distance, i) for i in devices if i - distance in devices]
    return lax.ppermute(block, axis, route)


def lagrange_rows(points, gll_points):
    values = np.ones((points.shape[0], 5))
    for column in range(5):
        for other_node in range(5):
            if other_node != column:
                values[:, column] *= (points - gll_points[other_node]) / (
                    gll_points[column] - gll_points[other_node]
                )
    return values


def element_tables():
    root_value = math.sqrt(3.0 / 7.0)
    gll_points = np.array([-1.0, -root_value, 0.0, root_value, 1.0])
    gll_weights = np.array([0.1, 49.0 / 90.0, 32.0 / 45.0, 49.0 / 90.0, 0.1])
    identity_mask = np.arange(5)[:, None] == np.arange(5)[None, :]
    spread = gll_points[:, None] - gll_points[None, :]
    spread = np.where(identity_mask, 1.0, spread)
    factor = np.prod(spread, axis=1)
    derive = factor[:, None] / factor[None, :] / spread
    diag_values = np.sum(1.0 / spread, axis=1) - 1.0
    derive = np.where(identity_mask, diag_values[:, None], derive)
    stiff_line = derive.T @ (gll_weights[:, None] * derive)
    mass_line = np.where(identity_mask, gll_weights[None, :], 0.0)
    stiffness = (
        np.kron(np.kron(stiff_line, mass_line), mass_line)
        + np.kron(np.kron(mass_line, stiff_line), mass_line)
        + np.kron(np.kron(mass_line, mass_line), stiff_line)
    )
    extract = np.zeros((150, 125))
    face_weight = np.zeros((6, 25))
    face_nodes = np.zeros((6, 25), np.int64)
    for normal in range(3):
        for side_pick in range(2):
            face_id = 2 * normal + side_pick
            for first_pos in range(5):
                for second_pos in range(5):
                    triple = [first_pos, second_pos]
                    triple.insert(normal, 4 * side_pick)
                    node_id = 25 * triple[0] + 5 * triple[1] + triple[2]
                    extract[25 * face_id + 5 * first_pos + second_pos, node_id] = 1.0
                    face_nodes[face_id, 5 * first_pos + second_pos] = node_id
                    face_weight[face_id, 5 * first_pos + second_pos] = (
                        gll_weights[first_pos] * gll_weights[second_pos]
                    )
    face_diag = extract.T @ face_weight.reshape(150)
    node_range = np.arange(125)
    stiff_diag = stiffness[node_range, node_range].copy()
    upper_bound = max(2.0, float(np.max(np.sum(np.abs(stiffness), axis=1) / stiff_diag)))
    halves = np.stack(
        [
            lagrange_rows((gll_points - 1.0) / 2.0, gll_points),
            lagrange_rows((gll_points + 1.0) / 2.0, gll_points),
        ]
    )
    return (stiffness, extract, face_weight, face_diag, stiff_diag, upper_bound, halves, face_nodes)


def to_bf16_grid(values):
    return lax.reduce_precision(values, exponent_bits=8, mantissa_bits=7)


def split3(values):
    high = to_bf16_grid(values)
    rest = values - high
    middle = to_bf16_grid(rest)
    low = rest - middle
    return tuple(part.astype(jnp.bfloat16) for part in (high, middle, low))


def place(onehot, values):
    rows, lanes = values.shape
    width = -(-lanes // 128) * 128
    parts = [jnp.pad(part, ((0, 0), (0, width - lanes))) for part in split3(values)]
    out = jnp.dot(onehot, jnp.concatenate(parts, axis=1), preferred_element_type=jnp.float32)
    total = (out[:, :width] + out[:, width : 2 * width]) + out[:, 2 * width :]
    return total[:, :lanes]


def chebyshev(start, residual_now, operator_fn, inverse_diag, upper_bound, keep_last):
    low_end = upper_bound * lower_share
    center = 0.5 * (upper_bound + low_end)
    radius = 0.5 * (upper_bound - low_end)
    sigma_value = center / radius
    rho_value = 1.0 / sigma_value
    solution = start
    update = inverse_diag * residual_now / center
    for turn_index in range(3):
        solution = solution + update
        if turn_index < 2 or keep_last:
            residual_now = residual_now - operator_fn(update)
        if turn_index < 2:
            rho_next = 1.0 / (2.0 * sigma_value - rho_value)
            update = (
                rho_next * rho_value * update
                + 2.0 * rho_next / radius * inverse_diag * residual_now
            )
            rho_value = rho_next
    return (solution, residual_now)


def onehot_of(rows_ids, column_ids):
    return (rows_ids[:, None] == column_ids[None, :]).astype(jnp.bfloat16)


def level_plan(local_ids, left_ids, right_ids, weight):
    face_count = local_ids.shape[0]
    elem_count = face_count // 6
    has_local = local_ids >= 0
    source = jnp.where(has_local, local_ids, 0)
    send_ids = jnp.concatenate([left_ids, right_ids])
    onehot = onehot_of(jnp.arange(face_count, dtype=jnp.int32), send_ids)
    face_w = jnp.broadcast_to(weight[:, None, :], (6, elem_count, 25)).reshape(face_count, 25)
    local_w = jnp.where(has_local[:, None], face_w, 0.0)
    return source, send_ids, onehot, face_w, local_w


def place_packed(onehot, values):
    high, middle, low = split3(values[:, :25])
    gap = jnp.zeros((values.shape[0], 7), jnp.bfloat16)
    tail = jnp.zeros((values.shape[0], 39), jnp.bfloat16)
    packed = jnp.concatenate([high, gap, middle, gap, low, tail], axis=1)
    out = jnp.dot(onehot, packed, preferred_element_type=jnp.float32)
    return (out[:, 0:25] + out[:, 32:57]) + out[:, 64:89]


def apply_level(vector_t, scale_col, plan, mats):
    source, send_ids, onehot, face_w, local_w = plan
    stiffness_t, pick, fold = mats
    elem_count = vector_t.shape[0]
    shared = send_ids.shape[0] // 2
    faces = jnp.concatenate(
        [jnp.dot(vector_t, pick[f], precision=highest) for f in range(6)], axis=0
    )
    sent = faces[send_ids]
    from_left = passed_along(sent[shared:], AXES, 1)
    from_right = passed_along(sent[:shared], AXES, -1)
    local = faces[source]
    received = jnp.concatenate([from_left, from_right], axis=0)
    boundary = place_packed(onehot, received)
    jump = (faces[:, :25] - boundary) * face_w - local[:, :25] * local_w
    folded = lax.dot_general(
        jump.reshape(6, elem_count, 25), fold, (((2,), (1,)), ((0,), (0,))), precision=highest
    ).sum(axis=0)
    interior = scale_col * jnp.dot(vector_t, stiffness_t, precision=highest)
    return interior + folded


def interpolate_t(values_t, code_row, mats):
    mixed = jnp.dot(values_t, mats, precision=highest)
    out = jnp.zeros_like(values_t)
    for q in range(9):
        out = jnp.where(code_row[:, None] == q, mixed[:, 128 * q : 128 * q + 125], out)
    return out


def on_device(
    load_vector,
    fine_scale,
    coarse_scale,
    parent_owner,
    parent_pos,
    child_code,
    arrival_slot,
    fine_local,
    fine_left,
    fine_right,
    coarse_local,
    coarse_left,
    coarse_right,
):
    stiffness, extract, face_weight, face_diag, stiff_diag, upper_bound, halves, face_nodes = (
        element_tables()
    )
    pick = np.zeros((6, 125, 128))
    fold = np.zeros((6, 25, 125))
    weight = np.zeros((6, 25))
    for f in range(6):
        for m in range(25):
            pick[f, face_nodes[f, m], m] = 1.0
            fold[f, m, face_nodes[f, m]] = penalty_weight
            weight[f, m] = face_weight[f, m]
    prolong = np.zeros((125, 9 * 128))
    restrict = np.zeros((125, 9 * 128))
    for q in range(9):
        if q == 8:
            matrix = np.eye(125)
        else:
            matrix = np.kron(np.kron(halves[(q // 4) % 2], halves[(q // 2) % 2]), halves[q % 2])
        prolong[:, 128 * q : 128 * q + 125] = matrix.T
        restrict[:, 128 * q : 128 * q + 125] = matrix
    f32 = lambda a: jnp.asarray(a, jnp.float32)
    mats = (f32(stiffness.T), f32(pick), f32(fold))
    weight = f32(weight)
    prolong = f32(prolong)
    restrict = f32(restrict)
    face_diag = f32(face_diag)
    stiff_diag = f32(stiff_diag)

    fine_plan = level_plan(fine_local, fine_left, fine_right, weight)
    coarse_plan = level_plan(coarse_local, coarse_left, coarse_right, weight)
    fine_col = fine_scale[:, None]
    coarse_col = coarse_scale[:, None]

    def fine_apply(vector_t):
        return apply_level(vector_t, fine_col, fine_plan, mats)

    def coarse_apply(vector_t):
        return apply_level(vector_t, coarse_col, coarse_plan, mats)

    def inverse_diagonal(scale_col):
        return 1.0 / (scale_col * stiff_diag[None, :] + penalty_weight * face_diag[None, :])

    fine_inverse = inverse_diagonal(fine_col)
    coarse_inverse = inverse_diagonal(coarse_col)
    load_t = load_vector.T
    first_x, first_r = chebyshev(
        jnp.zeros_like(load_t), load_t, fine_apply, fine_inverse, upper_bound, True
    )
    rank_count = lax.axis_size(AXES)
    slot_count = arrival_slot.shape[0]
    capacity = slot_count // rank_count
    coarse_count = coarse_scale.shape[0]
    target = parent_owner * capacity + parent_pos
    slot_ids = jnp.arange(slot_count, dtype=jnp.int32)
    coarse_ids = jnp.arange(coarse_count, dtype=jnp.int32)

    pieces = interpolate_t(first_r, child_code, restrict)
    buffer = place(onehot_of(slot_ids, target), pieces)
    arrived = lax.all_to_all(buffer, AXES, 0, 0, tiled=True)
    coarse_rhs = place(onehot_of(coarse_ids, arrival_slot), arrived)
    coarse_x, unused_r = chebyshev(
        jnp.zeros_like(coarse_rhs), coarse_rhs, coarse_apply, coarse_inverse, upper_bound, False
    )
    filled = place(onehot_of(arrival_slot, coarse_ids), coarse_x)
    returned = lax.all_to_all(filled, AXES, 0, 0, tiled=True)
    correction = interpolate_t(place(onehot_of(target, slot_ids), returned), child_code, prolong)
    second_x = first_x + correction
    second_r = first_r - fine_apply(correction)
    final_x, final_r = chebyshev(second_x, second_r, fine_apply, fine_inverse, upper_bound, True)
    return (final_x.T, final_r.T)


def solution(mesh):
    in_specs = (P(None, AXES),) + (P(AXES),) * 12
    out_specs = (P(None, AXES), P(None, AXES))
    return jax.shard_map(
        on_device, mesh=mesh, in_specs=in_specs, out_specs=out_specs, check_vma=False
    )
```

```python
import math

import jax
import jax.numpy as jnp
import numpy as np
from jax import lax
from jax.sharding import PartitionSpec as P

highest = lax.Precision.HIGHEST
penalty_weight = 20.0
lower_share = 0.125
AXES = ("elem", "sub")


def passed_along(block, axis, distance):
    devices = range(lax.axis_size(axis))
    route = [(i - distance, i) for i in devices if i - distance in devices]
    return lax.ppermute(block, axis, route)


def lagrange_rows(points, gll_points):
    values = np.ones((points.shape[0], 5))
    for column in range(5):
        for other_node in range(5):
            if other_node != column:
                values[:, column] *= (points - gll_points[other_node]) / (
                    gll_points[column] - gll_points[other_node]
                )
    return values


def element_tables():
    root_value = math.sqrt(3.0 / 7.0)
    gll_points = np.array([-1.0, -root_value, 0.0, root_value, 1.0])
    gll_weights = np.array([0.1, 49.0 / 90.0, 32.0 / 45.0, 49.0 / 90.0, 0.1])
    identity_mask = np.arange(5)[:, None] == np.arange(5)[None, :]
    spread = gll_points[:, None] - gll_points[None, :]
    spread = np.where(identity_mask, 1.0, spread)
    factor = np.prod(spread, axis=1)
    derive = factor[:, None] / factor[None, :] / spread
    diag_values = np.sum(1.0 / spread, axis=1) - 1.0
    derive = np.where(identity_mask, diag_values[:, None], derive)
    stiff_line = derive.T @ (gll_weights[:, None] * derive)
    mass_line = np.where(identity_mask, gll_weights[None, :], 0.0)
    stiffness = (
        np.kron(np.kron(stiff_line, mass_line), mass_line)
        + np.kron(np.kron(mass_line, stiff_line), mass_line)
        + np.kron(np.kron(mass_line, mass_line), stiff_line)
    )
    extract = np.zeros((150, 125))
    face_weight = np.zeros((6, 25))
    face_nodes = np.zeros((6, 25), np.int64)
    for normal in range(3):
        for side_pick in range(2):
            face_id = 2 * normal + side_pick
            for first_pos in range(5):
                for second_pos in range(5):
                    triple = [first_pos, second_pos]
                    triple.insert(normal, 4 * side_pick)
                    node_id = 25 * triple[0] + 5 * triple[1] + triple[2]
                    extract[25 * face_id + 5 * first_pos + second_pos, node_id] = 1.0
                    face_nodes[face_id, 5 * first_pos + second_pos] = node_id
                    face_weight[face_id, 5 * first_pos + second_pos] = (
                        gll_weights[first_pos] * gll_weights[second_pos]
                    )
    face_diag = extract.T @ face_weight.reshape(150)
    node_range = np.arange(125)
    stiff_diag = stiffness[node_range, node_range].copy()
    upper_bound = max(2.0, float(np.max(np.sum(np.abs(stiffness), axis=1) / stiff_diag)))
    halves = np.stack(
        [
            lagrange_rows((gll_points - 1.0) / 2.0, gll_points),
            lagrange_rows((gll_points + 1.0) / 2.0, gll_points),
        ]
    )
    return (stiffness, extract, face_weight, face_diag, stiff_diag, upper_bound, halves, face_nodes)


def to_bf16_grid(values):
    return lax.reduce_precision(values, exponent_bits=8, mantissa_bits=7)


def split3(values):
    high = to_bf16_grid(values)
    rest = values - high
    middle = to_bf16_grid(rest)
    low = rest - middle
    return tuple(part.astype(jnp.bfloat16) for part in (high, middle, low))


def place(onehot, values):
    rows, lanes = values.shape
    width = -(-lanes // 128) * 128
    parts = [jnp.pad(part, ((0, 0), (0, width - lanes))) for part in split3(values)]
    out = jnp.dot(onehot, jnp.concatenate(parts, axis=1), preferred_element_type=jnp.float32)
    total = (out[:, :width] + out[:, width : 2 * width]) + out[:, 2 * width :]
    return total[:, :lanes]


def chebyshev(start, residual_now, operator_fn, inverse_diag, upper_bound, keep_last):
    low_end = upper_bound * lower_share
    center = 0.5 * (upper_bound + low_end)
    radius = 0.5 * (upper_bound - low_end)
    sigma_value = center / radius
    rho_value = 1.0 / sigma_value
    solution = start
    update = inverse_diag * residual_now / center
    for turn_index in range(3):
        solution = solution + update
        if turn_index < 2 or keep_last:
            residual_now = residual_now - operator_fn(update)
        if turn_index < 2:
            rho_next = 1.0 / (2.0 * sigma_value - rho_value)
            update = (
                rho_next * rho_value * update
                + 2.0 * rho_next / radius * inverse_diag * residual_now
            )
            rho_value = rho_next
    return (solution, residual_now)


def onehot_of(rows_ids, column_ids):
    return (rows_ids[:, None] == column_ids[None, :]).astype(jnp.bfloat16)


def level_plan(local_ids, left_ids, right_ids):
    face_count = local_ids.shape[0]
    shared = left_ids.shape[0]
    zero_row = face_count + 2 * shared
    source = jnp.where(local_ids >= 0, local_ids, zero_row)
    lanes = jnp.arange(shared, dtype=jnp.int32)
    source = source.at[left_ids].set(face_count + lanes).at[right_ids].set(face_count + shared + lanes)
    send_ids = jnp.concatenate([left_ids, right_ids])
    return source, send_ids


def apply_level(vector_t, scale_col, plan, mats):
    source, send_ids = plan
    stiffness_t, pick, fold, weight = mats
    elem_count = vector_t.shape[0]
    shared = send_ids.shape[0] // 2
    faces = jnp.concatenate(
        [jnp.dot(vector_t, pick[f], precision=highest) for f in range(6)], axis=0
    )
    sent = faces[send_ids]
    from_left = passed_along(sent[shared:], AXES, 1)
    from_right = passed_along(sent[:shared], AXES, -1)
    extended = jnp.concatenate(
        [faces, from_left, from_right, jnp.zeros((8, faces.shape[1]), faces.dtype)], axis=0
    )
    partner = extended[source]
    jump = (faces - partner).reshape(6, elem_count, 128) * weight[:, None, :]
    folded = lax.dot_general(
        jump, fold, (((2,), (1,)), ((0,), (0,))), precision=highest
    ).sum(axis=0)
    interior = scale_col * jnp.dot(vector_t, stiffness_t, precision=highest)
    return interior + folded


def interpolate_t(values_t, code_row, mats):
    mixed = jnp.dot(values_t, mats, precision=highest)
    out = jnp.zeros_like(values_t)
    for q in range(9):
        out = jnp.where(code_row[:, None] == q, mixed[:, 128 * q : 128 * q + 125], out)
    return out


def on_device(
    load_vector,
    fine_scale,
    coarse_scale,
    parent_owner,
    parent_pos,
    child_code,
    arrival_slot,
    fine_local,
    fine_left,
    fine_right,
    coarse_local,
    coarse_left,
    coarse_right,
):
    stiffness, extract, face_weight, face_diag, stiff_diag, upper_bound, halves, face_nodes = (
        element_tables()
    )
    pick = np.zeros((6, 125, 128))
    fold = np.zeros((6, 128, 125))
    weight = np.zeros((6, 128))
    for f in range(6):
        for m in range(25):
            pick[f, face_nodes[f, m], m] = 1.0
            fold[f, m, face_nodes[f, m]] = penalty_weight
            weight[f, m] = face_weight[f, m]
    prolong = np.zeros((125, 9 * 128))
    restrict = np.zeros((125, 9 * 128))
    for q in range(9):
        if q == 8:
            matrix = np.eye(125)
        else:
            matrix = np.kron(np.kron(halves[(q // 4) % 2], halves[(q // 2) % 2]), halves[q % 2])
        prolong[:, 128 * q : 128 * q + 125] = matrix.T
        restrict[:, 128 * q : 128 * q + 125] = matrix
    f32 = lambda a: jnp.asarray(a, jnp.float32)
    mats = (f32(stiffness.T), f32(pick), f32(fold), f32(weight))
    prolong = f32(prolong)
    restrict = f32(restrict)
    face_diag = f32(face_diag)
    stiff_diag = f32(stiff_diag)

    fine_plan = level_plan(fine_local, fine_left, fine_right)
    coarse_plan = level_plan(coarse_local, coarse_left, coarse_right)
    fine_col = fine_scale[:, None]
    coarse_col = coarse_scale[:, None]

    def fine_apply(vector_t):
        return apply_level(vector_t, fine_col, fine_plan, mats)

    def coarse_apply(vector_t):
        return apply_level(vector_t, coarse_col, coarse_plan, mats)

    def inverse_diagonal(scale_col):
        return 1.0 / (scale_col * stiff_diag[None, :] + penalty_weight * face_diag[None, :])

    fine_inverse = inverse_diagonal(fine_col)
    coarse_inverse = inverse_diagonal(coarse_col)
    load_t = load_vector.T
    first_x, first_r = chebyshev(
        jnp.zeros_like(load_t), load_t, fine_apply, fine_inverse, upper_bound, True
    )
    rank_count = lax.axis_size(AXES)
    slot_count = arrival_slot.shape[0]
    capacity = slot_count // rank_count
    coarse_count = coarse_scale.shape[0]
    target = parent_owner * capacity + parent_pos
    slot_ids = jnp.arange(slot_count, dtype=jnp.int32)
    coarse_ids = jnp.arange(coarse_count, dtype=jnp.int32)

    pieces = interpolate_t(first_r, child_code, restrict)
    buffer = place(onehot_of(slot_ids, target), pieces)
    arrived = lax.all_to_all(buffer, AXES, 0, 0, tiled=True)
    coarse_rhs = place(onehot_of(coarse_ids, arrival_slot), arrived)
    coarse_x, unused_r = chebyshev(
        jnp.zeros_like(coarse_rhs), coarse_rhs, coarse_apply, coarse_inverse, upper_bound, False
    )
    filled = place(onehot_of(arrival_slot, coarse_ids), coarse_x)
    returned = lax.all_to_all(filled, AXES, 0, 0, tiled=True)
    correction = interpolate_t(place(onehot_of(target, slot_ids), returned), child_code, prolong)
    second_x = first_x + correction
    second_r = first_r - fine_apply(correction)
    final_x, final_r = chebyshev(second_x, second_r, fine_apply, fine_inverse, upper_bound, True)
    return (final_x.T, final_r.T)


def solution(mesh):
    in_specs = (P(None, AXES),) + (P(AXES),) * 12
    out_specs = (P(None, AXES), P(None, AXES))
    return jax.shard_map(
        on_device, mesh=mesh, in_specs=in_specs, out_specs=out_specs, check_vma=False
    )
```

```python
import math

import jax
import jax.numpy as jnp
import numpy as np
from jax import lax
from jax.sharding import PartitionSpec as P

highest = lax.Precision.HIGHEST
penalty_weight = 20.0
lower_share = 0.125
AXES = ("elem", "sub")


def passed_along(block, axis, distance):
    devices = range(lax.axis_size(axis))
    route = [(i - distance, i) for i in devices if i - distance in devices]
    return lax.ppermute(block, axis, route)


def lagrange_rows(points, gll_points):
    values = np.ones((points.shape[0], 5))
    for column in range(5):
        for other_node in range(5):
            if other_node != column:
                values[:, column] *= (points - gll_points[other_node]) / (
                    gll_points[column] - gll_points[other_node]
                )
    return values


def element_tables():
    root_value = math.sqrt(3.0 / 7.0)
    gll_points = np.array([-1.0, -root_value, 0.0, root_value, 1.0])
    gll_weights = np.array([0.1, 49.0 / 90.0, 32.0 / 45.0, 49.0 / 90.0, 0.1])
    identity_mask = np.arange(5)[:, None] == np.arange(5)[None, :]
    spread = gll_points[:, None] - gll_points[None, :]
    spread = np.where(identity_mask, 1.0, spread)
    factor = np.prod(spread, axis=1)
    derive = factor[:, None] / factor[None, :] / spread
    diag_values = np.sum(1.0 / spread, axis=1) - 1.0
    derive = np.where(identity_mask, diag_values[:, None], derive)
    stiff_line = derive.T @ (gll_weights[:, None] * derive)
    mass_line = np.where(identity_mask, gll_weights[None, :], 0.0)
    stiffness = (
        np.kron(np.kron(stiff_line, mass_line), mass_line)
        + np.kron(np.kron(mass_line, stiff_line), mass_line)
        + np.kron(np.kron(mass_line, mass_line), stiff_line)
    )
    extract = np.zeros((150, 125))
    face_weight = np.zeros((6, 25))
    face_nodes = np.zeros((6, 25), np.int64)
    for normal in range(3):
        for side_pick in range(2):
            face_id = 2 * normal + side_pick
            for first_pos in range(5):
                for second_pos in range(5):
                    triple = [first_pos, second_pos]
                    triple.insert(normal, 4 * side_pick)
                    node_id = 25 * triple[0] + 5 * triple[1] + triple[2]
                    extract[25 * face_id + 5 * first_pos + second_pos, node_id] = 1.0
                    face_nodes[face_id, 5 * first_pos + second_pos] = node_id
                    face_weight[face_id, 5 * first_pos + second_pos] = (
                        gll_weights[first_pos] * gll_weights[second_pos]
                    )
    face_diag = extract.T @ face_weight.reshape(150)
    node_range = np.arange(125)
    stiff_diag = stiffness[node_range, node_range].copy()
    upper_bound = max(2.0, float(np.max(np.sum(np.abs(stiffness), axis=1) / stiff_diag)))
    halves = np.stack(
        [
            lagrange_rows((gll_points - 1.0) / 2.0, gll_points),
            lagrange_rows((gll_points + 1.0) / 2.0, gll_points),
        ]
    )
    return (stiffness, extract, face_weight, face_diag, stiff_diag, upper_bound, halves, face_nodes)


def to_bf16_grid(values):
    return lax.reduce_precision(values, exponent_bits=8, mantissa_bits=7)


def split3(values):
    high = to_bf16_grid(values)
    rest = values - high
    middle = to_bf16_grid(rest)
    low = rest - middle
    return tuple(part.astype(jnp.bfloat16) for part in (high, middle, low))


def place(onehot, values):
    rows, lanes = values.shape
    width = -(-lanes // 128) * 128
    parts = [jnp.pad(part, ((0, 0), (0, width - lanes))) for part in split3(values)]
    out = jnp.dot(onehot, jnp.concatenate(parts, axis=1), preferred_element_type=jnp.float32)
    total = (out[:, :width] + out[:, width : 2 * width]) + out[:, 2 * width :]
    return total[:, :lanes]


def chebyshev(start, residual_now, operator_fn, inverse_diag, upper_bound, keep_last):
    low_end = upper_bound * lower_share
    center = 0.5 * (upper_bound + low_end)
    radius = 0.5 * (upper_bound - low_end)
    sigma_value = center / radius
    rho_value = 1.0 / sigma_value
    solution = start
    update = inverse_diag * residual_now / center
    for turn_index in range(3):
        solution = solution + update
        if turn_index < 2 or keep_last:
            residual_now = residual_now - operator_fn(update)
        if turn_index < 2:
            rho_next = 1.0 / (2.0 * sigma_value - rho_value)
            update = (
                rho_next * rho_value * update
                + 2.0 * rho_next / radius * inverse_diag * residual_now
            )
            rho_value = rho_next
    return (solution, residual_now)


def onehot_of(rows_ids, column_ids):
    return (rows_ids[:, None] == column_ids[None, :]).astype(jnp.bfloat16)


def level_plan(local_ids, left_ids, right_ids):
    face_count = local_ids.shape[0]
    elem_count = face_count // 6
    has_local = local_ids >= 0
    source = jnp.where(has_local, local_ids, 0)
    send_ids = jnp.concatenate([left_ids, right_ids])
    face_of = send_ids // elem_count
    block_of = jnp.arange(6 * 128, dtype=jnp.int32) // 128
    in_block = face_of[:, None] == block_of[None, :]
    onehot = onehot_of(jnp.arange(elem_count, dtype=jnp.int32), send_ids % elem_count)
    return has_local, source, send_ids, in_block, onehot


def apply_level(vector_t, scale_col, plan, mats):
    has_local, source, send_ids, in_block, onehot = plan
    stiffness_t, pick, fold, weight = mats
    elem_count = vector_t.shape[0]
    shared = send_ids.shape[0] // 2
    faces = jnp.concatenate(
        [jnp.dot(vector_t, pick[f], precision=highest) for f in range(6)], axis=0
    )
    sent = faces[send_ids]
    from_left = passed_along(sent[shared:], AXES, 1)
    from_right = passed_along(sent[:shared], AXES, -1)
    partner = jnp.where(has_local[:, None], faces[source], 0.0)
    jump = (faces - partner).reshape(6, elem_count, 128) * weight[:, None, :]
    folded = lax.dot_general(
        jump, fold, (((2,), (1,)), ((0,), (0,))), precision=highest
    ).sum(axis=0)
    received = jnp.concatenate([from_left, from_right], axis=0)
    spread = jnp.where(in_block, jnp.tile(received, (1, 6)) * weight.reshape(1, 6 * 128), 0.0)
    shared_terms = jnp.dot(spread, fold.reshape(6 * 128, 125), precision=highest)
    interior = scale_col * jnp.dot(vector_t, stiffness_t, precision=highest)
    return (interior + folded) - place(onehot, shared_terms)


def interpolate_t(values_t, code_row, mats):
    mixed = jnp.dot(values_t, mats, precision=highest)
    out = jnp.zeros_like(values_t)
    for q in range(9):
        out = jnp.where(code_row[:, None] == q, mixed[:, 128 * q : 128 * q + 125], out)
    return out


def on_device(
    load_vector,
    fine_scale,
    coarse_scale,
    parent_owner,
    parent_pos,
    child_code,
    arrival_slot,
    fine_local,
    fine_left,
    fine_right,
    coarse_local,
    coarse_left,
    coarse_right,
):
    stiffness, extract, face_weight, face_diag, stiff_diag, upper_bound, halves, face_nodes = (
        element_tables()
    )
    pick = np.zeros((6, 125, 128))
    fold = np.zeros((6, 128, 125))
    weight = np.zeros((6, 128))
    for f in range(6):
        for m in range(25):
            pick[f, face_nodes[f, m], m] = 1.0
            fold[f, m, face_nodes[f, m]] = penalty_weight
            weight[f, m] = face_weight[f, m]
    prolong = np.zeros((125, 9 * 128))
    restrict = np.zeros((125, 9 * 128))
    for q in range(9):
        if q == 8:
            matrix = np.eye(125)
        else:
            matrix = np.kron(np.kron(halves[(q // 4) % 2], halves[(q // 2) % 2]), halves[q % 2])
        prolong[:, 128 * q : 128 * q + 125] = matrix.T
        restrict[:, 128 * q : 128 * q + 125] = matrix
    f32 = lambda a: jnp.asarray(a, jnp.float32)
    mats = (f32(stiffness.T), f32(pick), f32(fold), f32(weight))
    prolong = f32(prolong)
    restrict = f32(restrict)
    face_diag = f32(face_diag)
    stiff_diag = f32(stiff_diag)

    fine_plan = level_plan(fine_local, fine_left, fine_right)
    coarse_plan = level_plan(coarse_local, coarse_left, coarse_right)
    fine_col = fine_scale[:, None]
    coarse_col = coarse_scale[:, None]

    def fine_apply(vector_t):
        return apply_level(vector_t, fine_col, fine_plan, mats)

    def coarse_apply(vector_t):
        return apply_level(vector_t, coarse_col, coarse_plan, mats)

    def inverse_diagonal(scale_col):
        return 1.0 / (scale_col * stiff_diag[None, :] + penalty_weight * face_diag[None, :])

    fine_inverse = inverse_diagonal(fine_col)
    coarse_inverse = inverse_diagonal(coarse_col)
    load_t = load_vector.T
    first_x, first_r = chebyshev(
        jnp.zeros_like(load_t), load_t, fine_apply, fine_inverse, upper_bound, True
    )
    rank_count = lax.axis_size(AXES)
    slot_count = arrival_slot.shape[0]
    capacity = slot_count // rank_count
    coarse_count = coarse_scale.shape[0]
    target = parent_owner * capacity + parent_pos
    slot_ids = jnp.arange(slot_count, dtype=jnp.int32)
    coarse_ids = jnp.arange(coarse_count, dtype=jnp.int32)

    pieces = interpolate_t(first_r, child_code, restrict)
    buffer = place(onehot_of(slot_ids, target), pieces)
    arrived = lax.all_to_all(buffer, AXES, 0, 0, tiled=True)
    coarse_rhs = place(onehot_of(coarse_ids, arrival_slot), arrived)
    coarse_x, unused_r = chebyshev(
        jnp.zeros_like(coarse_rhs), coarse_rhs, coarse_apply, coarse_inverse, upper_bound, False
    )
    filled = place(onehot_of(arrival_slot, coarse_ids), coarse_x)
    returned = lax.all_to_all(filled, AXES, 0, 0, tiled=True)
    correction = interpolate_t(place(onehot_of(target, slot_ids), returned), child_code, prolong)
    second_x = first_x + correction
    second_r = first_r - fine_apply(correction)
    final_x, final_r = chebyshev(second_x, second_r, fine_apply, fine_inverse, upper_bound, True)
    return (final_x.T, final_r.T)


def solution(mesh):
    in_specs = (P(None, AXES),) + (P(AXES),) * 12
    out_specs = (P(None, AXES), P(None, AXES))
    return jax.shard_map(
        on_device, mesh=mesh, in_specs=in_specs, out_specs=out_specs, check_vma=False
    )
```

```python
import math

import jax
import jax.numpy as jnp
import numpy as np
from jax import lax
from jax.sharding import PartitionSpec as P

highest = lax.Precision.HIGHEST
penalty_weight = 20.0
lower_share = 0.125
AXES = ("elem", "sub")


def passed_along(block, axis, distance):
    devices = range(lax.axis_size(axis))
    route = [(i - distance, i) for i in devices if i - distance in devices]
    return lax.ppermute(block, axis, route)


def lagrange_rows(points, gll_points):
    values = np.ones((points.shape[0], 5))
    for column in range(5):
        for other_node in range(5):
            if other_node != column:
                values[:, column] *= (points - gll_points[other_node]) / (
                    gll_points[column] - gll_points[other_node]
                )
    return values


def element_tables():
    root_value = math.sqrt(3.0 / 7.0)
    gll_points = np.array([-1.0, -root_value, 0.0, root_value, 1.0])
    gll_weights = np.array([0.1, 49.0 / 90.0, 32.0 / 45.0, 49.0 / 90.0, 0.1])
    identity_mask = np.arange(5)[:, None] == np.arange(5)[None, :]
    spread = gll_points[:, None] - gll_points[None, :]
    spread = np.where(identity_mask, 1.0, spread)
    factor = np.prod(spread, axis=1)
    derive = factor[:, None] / factor[None, :] / spread
    diag_values = np.sum(1.0 / spread, axis=1) - 1.0
    derive = np.where(identity_mask, diag_values[:, None], derive)
    stiff_line = derive.T @ (gll_weights[:, None] * derive)
    mass_line = np.where(identity_mask, gll_weights[None, :], 0.0)
    stiffness = (
        np.kron(np.kron(stiff_line, mass_line), mass_line)
        + np.kron(np.kron(mass_line, stiff_line), mass_line)
        + np.kron(np.kron(mass_line, mass_line), stiff_line)
    )
    extract = np.zeros((150, 125))
    face_weight = np.zeros((6, 25))
    face_nodes = np.zeros((6, 25), np.int64)
    for normal in range(3):
        for side_pick in range(2):
            face_id = 2 * normal + side_pick
            for first_pos in range(5):
                for second_pos in range(5):
                    triple = [first_pos, second_pos]
                    triple.insert(normal, 4 * side_pick)
                    node_id = 25 * triple[0] + 5 * triple[1] + triple[2]
                    extract[25 * face_id + 5 * first_pos + second_pos, node_id] = 1.0
                    face_nodes[face_id, 5 * first_pos + second_pos] = node_id
                    face_weight[face_id, 5 * first_pos + second_pos] = (
                        gll_weights[first_pos] * gll_weights[second_pos]
                    )
    face_diag = extract.T @ face_weight.reshape(150)
    node_range = np.arange(125)
    stiff_diag = stiffness[node_range, node_range].copy()
    upper_bound = max(2.0, float(np.max(np.sum(np.abs(stiffness), axis=1) / stiff_diag)))
    halves = np.stack(
        [
            lagrange_rows((gll_points - 1.0) / 2.0, gll_points),
            lagrange_rows((gll_points + 1.0) / 2.0, gll_points),
        ]
    )
    return (stiffness, extract, face_weight, face_diag, stiff_diag, upper_bound, halves, face_nodes)


def to_bf16_grid(values):
    return lax.reduce_precision(values, exponent_bits=8, mantissa_bits=7)


def split3(values):
    high = to_bf16_grid(values)
    rest = values - high
    middle = to_bf16_grid(rest)
    low = rest - middle
    return tuple(part.astype(jnp.bfloat16) for part in (high, middle, low))


def place(onehot, values):
    rows, lanes = values.shape
    width = -(-lanes // 128) * 128
    parts = [jnp.pad(part, ((0, 0), (0, width - lanes))) for part in split3(values)]
    out = jnp.dot(onehot, jnp.concatenate(parts, axis=1), preferred_element_type=jnp.float32)
    total = (out[:, :width] + out[:, width : 2 * width]) + out[:, 2 * width :]
    return total[:, :lanes]


def chebyshev(start, residual_now, operator_fn, inverse_diag, upper_bound, keep_last):
    low_end = upper_bound * lower_share
    center = 0.5 * (upper_bound + low_end)
    radius = 0.5 * (upper_bound - low_end)
    sigma_value = center / radius
    rho_value = 1.0 / sigma_value
    solution = start
    update = inverse_diag * residual_now / center
    for turn_index in range(3):
        solution = solution + update
        if turn_index < 2 or keep_last:
            residual_now = residual_now - operator_fn(update)
        if turn_index < 2:
            rho_next = 1.0 / (2.0 * sigma_value - rho_value)
            update = (
                rho_next * rho_value * update
                + 2.0 * rho_next / radius * inverse_diag * residual_now
            )
            rho_value = rho_next
    return (solution, residual_now)


def onehot_of(rows_ids, column_ids):
    return (rows_ids[:, None] == column_ids[None, :]).astype(jnp.bfloat16)


def level_plan(local_ids, left_ids, right_ids):
    face_count = local_ids.shape[0]
    elem_count = face_count // 6
    source = jnp.where(local_ids >= 0, local_ids, face_count)
    send_ids = jnp.concatenate([right_ids, left_ids])
    shared_ids = jnp.concatenate([left_ids, right_ids])
    face_of = shared_ids // elem_count
    block_of = jnp.arange(6 * 128, dtype=jnp.int32) // 128
    in_block = face_of[:, None] == block_of[None, :]
    elem_ids = jnp.arange(elem_count, dtype=jnp.int32)
    onehot = (elem_ids[:, None] == (shared_ids % elem_count)[None, :]).astype(jnp.float32)
    return source, send_ids, in_block, onehot


def take_rows(table, rows):
    return table.at[rows].get(mode="promise_in_bounds")


def apply_level(vector_t, scale_col, plan, mats):
    source, send_ids, in_block, onehot = plan
    stiffness_t, pick, fold, weight = mats
    elem_count = vector_t.shape[0]
    face_count = 6 * elem_count
    shared = send_ids.shape[0] // 2
    faces = jnp.concatenate(
        [jnp.dot(vector_t, pick[f], precision=highest) for f in range(6)]
        + [jnp.zeros((8, 128), jnp.float32)],
        axis=0,
    )
    sent = take_rows(faces, send_ids)
    from_previous = passed_along(sent, AXES, 1)
    from_next = passed_along(sent, AXES, -1)
    partner = take_rows(faces, source)
    jump = (faces[:face_count] - partner).reshape(6, elem_count, 128) * weight[:, None, :]
    folded = lax.dot_general(
        jump, fold, (((2,), (1,)), ((0,), (0,))), precision=highest
    ).sum(axis=0)
    first_half = lax.broadcasted_iota(jnp.int32, sent.shape, 0) < shared
    received = jnp.where(first_half, from_previous, from_next)
    spread = jnp.where(in_block, jnp.tile(received, (1, 6)) * weight.reshape(1, 6 * 128), 0.0)
    shared_terms = jnp.dot(spread, fold.reshape(6 * 128, 125), precision=highest)
    interior = scale_col * jnp.dot(vector_t, stiffness_t, precision=highest)
    return (interior + folded) - jnp.dot(onehot, shared_terms, precision=highest)


def interpolate_t(values_t, code_row, mats):
    mixed = jnp.dot(values_t, mats, precision=highest)
    out = jnp.zeros_like(values_t)
    for q in range(9):
        out = jnp.where(code_row[:, None] == q, mixed[:, 128 * q : 128 * q + 125], out)
    return out


def on_device(
    load_vector,
    fine_scale,
    coarse_scale,
    parent_owner,
    parent_pos,
    child_code,
    arrival_slot,
    fine_local,
    fine_left,
    fine_right,
    coarse_local,
    coarse_left,
    coarse_right,
):
    stiffness, extract, face_weight, face_diag, stiff_diag, upper_bound, halves, face_nodes = (
        element_tables()
    )
    pick = np.zeros((6, 125, 128))
    fold = np.zeros((6, 128, 125))
    weight = np.zeros((6, 128))
    for f in range(6):
        for m in range(25):
            pick[f, face_nodes[f, m], m] = 1.0
            fold[f, m, face_nodes[f, m]] = penalty_weight
            weight[f, m] = face_weight[f, m]
    prolong = np.zeros((125, 9 * 128))
    restrict = np.zeros((125, 9 * 128))
    for q in range(9):
        if q == 8:
            matrix = np.eye(125)
        else:
            matrix = np.kron(np.kron(halves[(q // 4) % 2], halves[(q // 2) % 2]), halves[q % 2])
        prolong[:, 128 * q : 128 * q + 125] = matrix.T
        restrict[:, 128 * q : 128 * q + 125] = matrix
    f32 = lambda a: jnp.asarray(a, jnp.float32)
    mats = (f32(stiffness.T), f32(pick), f32(fold), f32(weight))
    prolong = f32(prolong)
    restrict = f32(restrict)
    face_diag = f32(face_diag)
    stiff_diag = f32(stiff_diag)

    fine_plan = level_plan(fine_local, fine_left, fine_right)
    coarse_plan = level_plan(coarse_local, coarse_left, coarse_right)
    fine_col = fine_scale[:, None]
    coarse_col = coarse_scale[:, None]

    def fine_apply(vector_t):
        return apply_level(vector_t, fine_col, fine_plan, mats)

    def coarse_apply(vector_t):
        return apply_level(vector_t, coarse_col, coarse_plan, mats)

    def inverse_diagonal(scale_col):
        return 1.0 / (scale_col * stiff_diag[None, :] + penalty_weight * face_diag[None, :])

    fine_inverse = inverse_diagonal(fine_col)
    coarse_inverse = inverse_diagonal(coarse_col)
    load_t = load_vector.T
    first_x, first_r = chebyshev(
        jnp.zeros_like(load_t), load_t, fine_apply, fine_inverse, upper_bound, True
    )
    rank_count = lax.axis_size(AXES)
    slot_count = arrival_slot.shape[0]
    capacity = slot_count // rank_count
    coarse_count = coarse_scale.shape[0]
    target = parent_owner * capacity + parent_pos
    slot_ids = jnp.arange(slot_count, dtype=jnp.int32)
    coarse_ids = jnp.arange(coarse_count, dtype=jnp.int32)

    pieces = interpolate_t(first_r, child_code, restrict)
    buffer = place(onehot_of(slot_ids, target), pieces)
    arrived = lax.all_to_all(buffer, AXES, 0, 0, tiled=True)
    coarse_rhs = place(onehot_of(coarse_ids, arrival_slot), arrived)
    coarse_x, unused_r = chebyshev(
        jnp.zeros_like(coarse_rhs), coarse_rhs, coarse_apply, coarse_inverse, upper_bound, False
    )
    filled = place(onehot_of(arrival_slot, coarse_ids), coarse_x)
    returned = lax.all_to_all(filled, AXES, 0, 0, tiled=True)
    correction = interpolate_t(place(onehot_of(target, slot_ids), returned), child_code, prolong)
    second_x = first_x + correction
    second_r = first_r - fine_apply(correction)
    final_x, final_r = chebyshev(second_x, second_r, fine_apply, fine_inverse, upper_bound, True)
    return (final_x.T, final_r.T)


def solution(mesh):
    in_specs = (P(None, AXES),) + (P(AXES),) * 12
    out_specs = (P(None, AXES), P(None, AXES))
    return jax.shard_map(
        on_device, mesh=mesh, in_specs=in_specs, out_specs=out_specs, check_vma=False
    )
```

```python
import math

import jax
import jax.numpy as jnp
import numpy as np
from jax import lax
from jax.sharding import PartitionSpec as P

highest = lax.Precision.HIGHEST
penalty_weight = 20.0
lower_share = 0.125
AXES = ("elem", "sub")


def passed_along(block, axis, distance):
    devices = range(lax.axis_size(axis))
    route = [(i - distance, i) for i in devices if i - distance in devices]
    return lax.ppermute(block, axis, route)


def lagrange_rows(points, gll_points):
    values = np.ones((points.shape[0], 5))
    for column in range(5):
        for other_node in range(5):
            if other_node != column:
                values[:, column] *= (points - gll_points[other_node]) / (
                    gll_points[column] - gll_points[other_node]
                )
    return values


def element_tables():
    root_value = math.sqrt(3.0 / 7.0)
    gll_points = np.array([-1.0, -root_value, 0.0, root_value, 1.0])
    gll_weights = np.array([0.1, 49.0 / 90.0, 32.0 / 45.0, 49.0 / 90.0, 0.1])
    identity_mask = np.arange(5)[:, None] == np.arange(5)[None, :]
    spread = gll_points[:, None] - gll_points[None, :]
    spread = np.where(identity_mask, 1.0, spread)
    factor = np.prod(spread, axis=1)
    derive = factor[:, None] / factor[None, :] / spread
    diag_values = np.sum(1.0 / spread, axis=1) - 1.0
    derive = np.where(identity_mask, diag_values[:, None], derive)
    stiff_line = derive.T @ (gll_weights[:, None] * derive)
    mass_line = np.where(identity_mask, gll_weights[None, :], 0.0)
    stiffness = (
        np.kron(np.kron(stiff_line, mass_line), mass_line)
        + np.kron(np.kron(mass_line, stiff_line), mass_line)
        + np.kron(np.kron(mass_line, mass_line), stiff_line)
    )
    extract = np.zeros((150, 125))
    face_weight = np.zeros((6, 25))
    face_nodes = np.zeros((6, 25), np.int64)
    for normal in range(3):
        for side_pick in range(2):
            face_id = 2 * normal + side_pick
            for first_pos in range(5):
                for second_pos in range(5):
                    triple = [first_pos, second_pos]
                    triple.insert(normal, 4 * side_pick)
                    node_id = 25 * triple[0] + 5 * triple[1] + triple[2]
                    extract[25 * face_id + 5 * first_pos + second_pos, node_id] = 1.0
                    face_nodes[face_id, 5 * first_pos + second_pos] = node_id
                    face_weight[face_id, 5 * first_pos + second_pos] = (
                        gll_weights[first_pos] * gll_weights[second_pos]
                    )
    face_diag = extract.T @ face_weight.reshape(150)
    node_range = np.arange(125)
    stiff_diag = stiffness[node_range, node_range].copy()
    upper_bound = max(2.0, float(np.max(np.sum(np.abs(stiffness), axis=1) / stiff_diag)))
    halves = np.stack(
        [
            lagrange_rows((gll_points - 1.0) / 2.0, gll_points),
            lagrange_rows((gll_points + 1.0) / 2.0, gll_points),
        ]
    )
    return (stiffness, extract, face_weight, face_diag, stiff_diag, upper_bound, halves, face_nodes)


def to_bf16_grid(values):
    return lax.reduce_precision(values, exponent_bits=8, mantissa_bits=7)


def split3(values):
    high = to_bf16_grid(values)
    rest = values - high
    middle = to_bf16_grid(rest)
    low = rest - middle
    return tuple(part.astype(jnp.bfloat16) for part in (high, middle, low))


def place(onehot, values):
    rows, lanes = values.shape
    width = -(-lanes // 128) * 128
    parts = [jnp.pad(part, ((0, 0), (0, width - lanes))) for part in split3(values)]
    out = jnp.dot(onehot, jnp.concatenate(parts, axis=1), preferred_element_type=jnp.float32)
    total = (out[:, :width] + out[:, width : 2 * width]) + out[:, 2 * width :]
    return total[:, :lanes]


def chebyshev(start, residual_now, operator_fn, inverse_diag, upper_bound, keep_last):
    low_end = upper_bound * lower_share
    center = 0.5 * (upper_bound + low_end)
    radius = 0.5 * (upper_bound - low_end)
    sigma_value = center / radius
    rho_value = 1.0 / sigma_value
    solution = start
    update = inverse_diag * residual_now / center
    for turn_index in range(3):
        solution = solution + update
        if turn_index < 2 or keep_last:
            residual_now = residual_now - operator_fn(update)
        if turn_index < 2:
            rho_next = 1.0 / (2.0 * sigma_value - rho_value)
            update = (
                rho_next * rho_value * update
                + 2.0 * rho_next / radius * inverse_diag * residual_now
            )
            rho_value = rho_next
    return (solution, residual_now)


def onehot_of(rows_ids, column_ids):
    return (rows_ids[:, None] == column_ids[None, :]).astype(jnp.bfloat16)


def level_plan(local_ids, left_ids, right_ids):
    face_count = local_ids.shape[0]
    elem_count = face_count // 6
    has_local = local_ids >= 0
    source = jnp.where(has_local, local_ids, 0)
    send_ids = jnp.concatenate([left_ids, right_ids])
    face_of = send_ids // elem_count
    block_of = jnp.arange(6 * 128, dtype=jnp.int32) // 128
    in_block = face_of[:, None] == block_of[None, :]
    onehot = onehot_of(jnp.arange(elem_count, dtype=jnp.int32), send_ids % elem_count)
    return has_local, source, send_ids, in_block, onehot


def apply_level(vector_t, scale_col, plan, mats):
    has_local, source, send_ids, in_block, onehot = plan
    stiffness_t, pick, fold, weight = mats
    elem_count = vector_t.shape[0]
    shared = send_ids.shape[0] // 2
    faces = jnp.concatenate(
        [jnp.dot(vector_t, pick[f], precision=highest) for f in range(6)], axis=0
    )
    sent = faces[send_ids]
    from_left = passed_along(sent[shared:], AXES, 1)
    from_right = passed_along(sent[:shared], AXES, -1)
    partner = jnp.where(has_local[:, None], faces[source], 0.0)
    jump = (faces - partner).reshape(6, elem_count, 128) * weight[:, None, :]
    folded = lax.dot_general(
        jump, fold, (((0, 2), (0, 1)), ((), ())), precision=lax.Precision.HIGH
    )
    received = jnp.concatenate([from_left, from_right], axis=0)
    spread = jnp.where(in_block, jnp.tile(received, (1, 6)) * weight.reshape(1, 6 * 128), 0.0)
    shared_terms = jnp.dot(spread, fold.reshape(6 * 128, 125), precision=highest)
    interior = scale_col * jnp.dot(vector_t, stiffness_t, precision=highest)
    return (interior + folded) - place(onehot, shared_terms)


def interpolate_t(values_t, code_row, mats):
    mixed = jnp.dot(values_t, mats, precision=highest)
    out = jnp.zeros_like(values_t)
    for q in range(9):
        out = jnp.where(code_row[:, None] == q, mixed[:, 128 * q : 128 * q + 125], out)
    return out


def on_device(
    load_vector,
    fine_scale,
    coarse_scale,
    parent_owner,
    parent_pos,
    child_code,
    arrival_slot,
    fine_local,
    fine_left,
    fine_right,
    coarse_local,
    coarse_left,
    coarse_right,
):
    stiffness, extract, face_weight, face_diag, stiff_diag, upper_bound, halves, face_nodes = (
        element_tables()
    )
    pick = np.zeros((6, 125, 128))
    fold = np.zeros((6, 128, 125))
    weight = np.zeros((6, 128))
    for f in range(6):
        for m in range(25):
            pick[f, face_nodes[f, m], m] = 1.0
            fold[f, m, face_nodes[f, m]] = penalty_weight
            weight[f, m] = face_weight[f, m]
    prolong = np.zeros((125, 9 * 128))
    restrict = np.zeros((125, 9 * 128))
    for q in range(9):
        if q == 8:
            matrix = np.eye(125)
        else:
            matrix = np.kron(np.kron(halves[(q // 4) % 2], halves[(q // 2) % 2]), halves[q % 2])
        prolong[:, 128 * q : 128 * q + 125] = matrix.T
        restrict[:, 128 * q : 128 * q + 125] = matrix
    f32 = lambda a: jnp.asarray(a, jnp.float32)
    mats = (f32(stiffness.T), f32(pick), f32(fold), f32(weight))
    prolong = f32(prolong)
    restrict = f32(restrict)
    face_diag = f32(face_diag)
    stiff_diag = f32(stiff_diag)

    fine_plan = level_plan(fine_local, fine_left, fine_right)
    coarse_plan = level_plan(coarse_local, coarse_left, coarse_right)
    fine_col = fine_scale[:, None]
    coarse_col = coarse_scale[:, None]

    def fine_apply(vector_t):
        return apply_level(vector_t, fine_col, fine_plan, mats)

    def coarse_apply(vector_t):
        return apply_level(vector_t, coarse_col, coarse_plan, mats)

    def inverse_diagonal(scale_col):
        return 1.0 / (scale_col * stiff_diag[None, :] + penalty_weight * face_diag[None, :])

    fine_inverse = inverse_diagonal(fine_col)
    coarse_inverse = inverse_diagonal(coarse_col)
    load_t = load_vector.T
    first_x, first_r = chebyshev(
        jnp.zeros_like(load_t), load_t, fine_apply, fine_inverse, upper_bound, True
    )
    rank_count = lax.axis_size(AXES)
    slot_count = arrival_slot.shape[0]
    capacity = slot_count // rank_count
    coarse_count = coarse_scale.shape[0]
    target = parent_owner * capacity + parent_pos
    slot_ids = jnp.arange(slot_count, dtype=jnp.int32)
    coarse_ids = jnp.arange(coarse_count, dtype=jnp.int32)

    pieces = interpolate_t(first_r, child_code, restrict)
    buffer = place(onehot_of(slot_ids, target), pieces)
    arrived = lax.all_to_all(buffer, AXES, 0, 0, tiled=True)
    coarse_rhs = place(onehot_of(coarse_ids, arrival_slot), arrived)
    coarse_x, unused_r = chebyshev(
        jnp.zeros_like(coarse_rhs), coarse_rhs, coarse_apply, coarse_inverse, upper_bound, False
    )
    filled = place(onehot_of(arrival_slot, coarse_ids), coarse_x)
    returned = lax.all_to_all(filled, AXES, 0, 0, tiled=True)
    correction = interpolate_t(place(onehot_of(target, slot_ids), returned), child_code, prolong)
    second_x = first_x + correction
    second_r = first_r - fine_apply(correction)
    final_x, final_r = chebyshev(second_x, second_r, fine_apply, fine_inverse, upper_bound, True)
    return (final_x.T, final_r.T)


def solution(mesh):
    in_specs = (P(None, AXES),) + (P(AXES),) * 12
    out_specs = (P(None, AXES), P(None, AXES))
    return jax.shard_map(
        on_device, mesh=mesh, in_specs=in_specs, out_specs=out_specs, check_vma=False
    )
```

```python
import math

import jax
import jax.numpy as jnp
import numpy as np
from jax import lax
from jax.sharding import PartitionSpec as P

highest = lax.Precision.HIGHEST
penalty_weight = 20.0
lower_share = 0.125
AXES = ("elem", "sub")


def passed_along(block, axis, distance):
    devices = range(lax.axis_size(axis))
    route = [(i - distance, i) for i in devices if i - distance in devices]
    return lax.ppermute(block, axis, route)


def lagrange_rows(points, gll_points):
    values = np.ones((points.shape[0], 5))
    for column in range(5):
        for other_node in range(5):
            if other_node != column:
                values[:, column] *= (points - gll_points[other_node]) / (
                    gll_points[column] - gll_points[other_node]
                )
    return values


def element_tables():
    root_value = math.sqrt(3.0 / 7.0)
    gll_points = np.array([-1.0, -root_value, 0.0, root_value, 1.0])
    gll_weights = np.array([0.1, 49.0 / 90.0, 32.0 / 45.0, 49.0 / 90.0, 0.1])
    identity_mask = np.arange(5)[:, None] == np.arange(5)[None, :]
    spread = gll_points[:, None] - gll_points[None, :]
    spread = np.where(identity_mask, 1.0, spread)
    factor = np.prod(spread, axis=1)
    derive = factor[:, None] / factor[None, :] / spread
    diag_values = np.sum(1.0 / spread, axis=1) - 1.0
    derive = np.where(identity_mask, diag_values[:, None], derive)
    stiff_line = derive.T @ (gll_weights[:, None] * derive)
    mass_line = np.where(identity_mask, gll_weights[None, :], 0.0)
    stiffness = (
        np.kron(np.kron(stiff_line, mass_line), mass_line)
        + np.kron(np.kron(mass_line, stiff_line), mass_line)
        + np.kron(np.kron(mass_line, mass_line), stiff_line)
    )
    extract = np.zeros((150, 125))
    face_weight = np.zeros((6, 25))
    face_nodes = np.zeros((6, 25), np.int64)
    for normal in range(3):
        for side_pick in range(2):
            face_id = 2 * normal + side_pick
            for first_pos in range(5):
                for second_pos in range(5):
                    triple = [first_pos, second_pos]
                    triple.insert(normal, 4 * side_pick)
                    node_id = 25 * triple[0] + 5 * triple[1] + triple[2]
                    extract[25 * face_id + 5 * first_pos + second_pos, node_id] = 1.0
                    face_nodes[face_id, 5 * first_pos + second_pos] = node_id
                    face_weight[face_id, 5 * first_pos + second_pos] = (
                        gll_weights[first_pos] * gll_weights[second_pos]
                    )
    face_diag = extract.T @ face_weight.reshape(150)
    node_range = np.arange(125)
    stiff_diag = stiffness[node_range, node_range].copy()
    upper_bound = max(2.0, float(np.max(np.sum(np.abs(stiffness), axis=1) / stiff_diag)))
    halves = np.stack(
        [
            lagrange_rows((gll_points - 1.0) / 2.0, gll_points),
            lagrange_rows((gll_points + 1.0) / 2.0, gll_points),
        ]
    )
    return (stiffness, extract, face_weight, face_diag, stiff_diag, upper_bound, halves, face_nodes)


def to_bf16_grid(values):
    return lax.reduce_precision(values, exponent_bits=8, mantissa_bits=7)


def split3(values):
    high = to_bf16_grid(values)
    rest = values - high
    middle = to_bf16_grid(rest)
    low = rest - middle
    return tuple(part.astype(jnp.bfloat16) for part in (high, middle, low))


def place(onehot, values):
    rows, lanes = values.shape
    width = -(-lanes // 128) * 128
    parts = [jnp.pad(part, ((0, 0), (0, width - lanes))) for part in split3(values)]
    out = jnp.dot(onehot, jnp.concatenate(parts, axis=1), preferred_element_type=jnp.float32)
    total = (out[:, :width] + out[:, width : 2 * width]) + out[:, 2 * width :]
    return total[:, :lanes]


def chebyshev(start, residual_now, operator_fn, inverse_diag, upper_bound, keep_last):
    low_end = upper_bound * lower_share
    center = 0.5 * (upper_bound + low_end)
    radius = 0.5 * (upper_bound - low_end)
    sigma_value = center / radius
    rho_value = 1.0 / sigma_value
    solution = start
    update = inverse_diag * residual_now / center
    for turn_index in range(3):
        solution = solution + update
        if turn_index < 2 or keep_last:
            residual_now = residual_now - operator_fn(update)
        if turn_index < 2:
            rho_next = 1.0 / (2.0 * sigma_value - rho_value)
            update = (
                rho_next * rho_value * update
                + 2.0 * rho_next / radius * inverse_diag * residual_now
            )
            rho_value = rho_next
    return (solution, residual_now)


def onehot_of(rows_ids, column_ids):
    return (rows_ids[:, None] == column_ids[None, :]).astype(jnp.bfloat16)


def level_plan(local_ids, left_ids, right_ids):
    face_count = local_ids.shape[0]
    elem_count = face_count // 6
    has_local = local_ids >= 0
    source = jnp.where(has_local, local_ids, 0)
    send_ids = jnp.concatenate([left_ids, right_ids])
    face_of = send_ids // elem_count
    block_of = jnp.arange(6 * 128, dtype=jnp.int32) // 128
    in_block = face_of[:, None] == block_of[None, :]
    onehot = onehot_of(jnp.arange(elem_count, dtype=jnp.int32), send_ids % elem_count)
    onehot = onehot.astype(jnp.float32)
    return has_local, source, send_ids, in_block, onehot


def apply_level(vector_t, scale_col, plan, mats):
    has_local, source, send_ids, in_block, onehot = plan
    stiffness_t, pick, fold, weight = mats
    elem_count = vector_t.shape[0]
    shared = send_ids.shape[0] // 2
    faces = jnp.concatenate(
        [jnp.dot(vector_t, pick[f], precision=highest) for f in range(6)], axis=0
    )
    from_left = passed_along(faces[send_ids[shared:]], AXES, 1)
    from_right = passed_along(faces[send_ids[:shared]], AXES, -1)
    partner = jnp.where(has_local[:, None], faces[source], 0.0)
    jump = (faces - partner).reshape(6, elem_count, 128) * weight[:, None, :]
    folded = lax.dot_general(
        jump, fold, (((0, 2), (0, 1)), ((), ())), precision=lax.Precision.HIGH
    )
    received = jnp.concatenate([from_left, from_right], axis=0)
    spread = jnp.where(in_block, jnp.tile(received, (1, 6)) * weight.reshape(1, 6 * 128), 0.0)
    shared_terms = jnp.dot(spread, fold.reshape(6 * 128, 125), precision=highest)
    interior = scale_col * jnp.dot(vector_t, stiffness_t, precision=highest)
    return (interior + folded) - jnp.dot(onehot, shared_terms, precision=highest)


def interpolate_t(values_t, code_row, mats):
    mixed = jnp.dot(values_t, mats, precision=highest)
    out = jnp.zeros_like(values_t)
    for q in range(9):
        out = jnp.where(code_row[:, None] == q, mixed[:, 128 * q : 128 * q + 125], out)
    return out


def on_device(
    load_vector,
    fine_scale,
    coarse_scale,
    parent_owner,
    parent_pos,
    child_code,
    arrival_slot,
    fine_local,
    fine_left,
    fine_right,
    coarse_local,
    coarse_left,
    coarse_right,
):
    stiffness, extract, face_weight, face_diag, stiff_diag, upper_bound, halves, face_nodes = (
        element_tables()
    )
    pick = np.zeros((6, 125, 128))
    fold = np.zeros((6, 128, 125))
    weight = np.zeros((6, 128))
    for f in range(6):
        for m in range(25):
            pick[f, face_nodes[f, m], m] = 1.0
            fold[f, m, face_nodes[f, m]] = penalty_weight
            weight[f, m] = face_weight[f, m]
    prolong = np.zeros((125, 9 * 128))
    restrict = np.zeros((125, 9 * 128))
    for q in range(9):
        if q == 8:
            matrix = np.eye(125)
        else:
            matrix = np.kron(np.kron(halves[(q // 4) % 2], halves[(q // 2) % 2]), halves[q % 2])
        prolong[:, 128 * q : 128 * q + 125] = matrix.T
        restrict[:, 128 * q : 128 * q + 125] = matrix
    f32 = lambda a: jnp.asarray(a, jnp.float32)
    mats = (f32(stiffness.T), f32(pick), f32(fold), f32(weight))
    prolong = f32(prolong)
    restrict = f32(restrict)
    face_diag = f32(face_diag)
    stiff_diag = f32(stiff_diag)

    fine_plan = level_plan(fine_local, fine_left, fine_right)
    coarse_plan = level_plan(coarse_local, coarse_left, coarse_right)
    fine_col = fine_scale[:, None]
    coarse_col = coarse_scale[:, None]

    def fine_apply(vector_t):
        return apply_level(vector_t, fine_col, fine_plan, mats)

    def coarse_apply(vector_t):
        return apply_level(vector_t, coarse_col, coarse_plan, mats)

    def inverse_diagonal(scale_col):
        return 1.0 / (scale_col * stiff_diag[None, :] + penalty_weight * face_diag[None, :])

    fine_inverse = inverse_diagonal(fine_col)
    coarse_inverse = inverse_diagonal(coarse_col)
    load_t = load_vector.T
    first_x, first_r = chebyshev(
        jnp.zeros_like(load_t), load_t, fine_apply, fine_inverse, upper_bound, True
    )
    rank_count = lax.axis_size(AXES)
    slot_count = arrival_slot.shape[0]
    capacity = slot_count // rank_count
    coarse_count = coarse_scale.shape[0]
    target = parent_owner * capacity + parent_pos
    slot_ids = jnp.arange(slot_count, dtype=jnp.int32)
    coarse_ids = jnp.arange(coarse_count, dtype=jnp.int32)

    pieces = interpolate_t(first_r, child_code, restrict)
    buffer = place(onehot_of(slot_ids, target), pieces)
    arrived = lax.all_to_all(buffer, AXES, 0, 0, tiled=True)
    coarse_rhs = place(onehot_of(coarse_ids, arrival_slot), arrived)
    coarse_x, unused_r = chebyshev(
        jnp.zeros_like(coarse_rhs), coarse_rhs, coarse_apply, coarse_inverse, upper_bound, False
    )
    filled = place(onehot_of(arrival_slot, coarse_ids), coarse_x)
    returned = lax.all_to_all(filled, AXES, 0, 0, tiled=True)
    correction = interpolate_t(place(onehot_of(target, slot_ids), returned), child_code, prolong)
    second_x = first_x + correction
    second_r = first_r - fine_apply(correction)
    final_x, final_r = chebyshev(second_x, second_r, fine_apply, fine_inverse, upper_bound, True)
    return (final_x.T, final_r.T)


def solution(mesh):
    in_specs = (P(None, AXES),) + (P(AXES),) * 12
    out_specs = (P(None, AXES), P(None, AXES))
    return jax.shard_map(
        on_device, mesh=mesh, in_specs=in_specs, out_specs=out_specs, check_vma=False
    )
```

```python
import math

import jax
import jax.numpy as jnp
import numpy as np
from jax import lax
from jax.sharding import PartitionSpec as P

highest = lax.Precision.HIGHEST
penalty_weight = 20.0
lower_share = 0.125
AXES = ("elem", "sub")


def passed_along(block, axis, distance):
    devices = range(lax.axis_size(axis))
    route = [(i - distance, i) for i in devices if i - distance in devices]
    return lax.ppermute(block, axis, route)


def lagrange_rows(points, gll_points):
    values = np.ones((points.shape[0], 5))
    for column in range(5):
        for other_node in range(5):
            if other_node != column:
                values[:, column] *= (points - gll_points[other_node]) / (
                    gll_points[column] - gll_points[other_node]
                )
    return values


def element_tables():
    root_value = math.sqrt(3.0 / 7.0)
    gll_points = np.array([-1.0, -root_value, 0.0, root_value, 1.0])
    gll_weights = np.array([0.1, 49.0 / 90.0, 32.0 / 45.0, 49.0 / 90.0, 0.1])
    identity_mask = np.arange(5)[:, None] == np.arange(5)[None, :]
    spread = gll_points[:, None] - gll_points[None, :]
    spread = np.where(identity_mask, 1.0, spread)
    factor = np.prod(spread, axis=1)
    derive = factor[:, None] / factor[None, :] / spread
    diag_values = np.sum(1.0 / spread, axis=1) - 1.0
    derive = np.where(identity_mask, diag_values[:, None], derive)
    stiff_line = derive.T @ (gll_weights[:, None] * derive)
    mass_line = np.where(identity_mask, gll_weights[None, :], 0.0)
    stiffness = (
        np.kron(np.kron(stiff_line, mass_line), mass_line)
        + np.kron(np.kron(mass_line, stiff_line), mass_line)
        + np.kron(np.kron(mass_line, mass_line), stiff_line)
    )
    extract = np.zeros((150, 125))
    face_weight = np.zeros((6, 25))
    face_nodes = np.zeros((6, 25), np.int64)
    for normal in range(3):
        for side_pick in range(2):
            face_id = 2 * normal + side_pick
            for first_pos in range(5):
                for second_pos in range(5):
                    triple = [first_pos, second_pos]
                    triple.insert(normal, 4 * side_pick)
                    node_id = 25 * triple[0] + 5 * triple[1] + triple[2]
                    extract[25 * face_id + 5 * first_pos + second_pos, node_id] = 1.0
                    face_nodes[face_id, 5 * first_pos + second_pos] = node_id
                    face_weight[face_id, 5 * first_pos + second_pos] = (
                        gll_weights[first_pos] * gll_weights[second_pos]
                    )
    face_diag = extract.T @ face_weight.reshape(150)
    node_range = np.arange(125)
    stiff_diag = stiffness[node_range, node_range].copy()
    upper_bound = max(2.0, float(np.max(np.sum(np.abs(stiffness), axis=1) / stiff_diag)))
    halves = np.stack(
        [
            lagrange_rows((gll_points - 1.0) / 2.0, gll_points),
            lagrange_rows((gll_points + 1.0) / 2.0, gll_points),
        ]
    )
    return (stiffness, extract, face_weight, face_diag, stiff_diag, upper_bound, halves, face_nodes)


def to_bf16_grid(values):
    return lax.reduce_precision(values, exponent_bits=8, mantissa_bits=7)


def split3(values):
    high = to_bf16_grid(values)
    rest = values - high
    middle = to_bf16_grid(rest)
    low = rest - middle
    return tuple(part.astype(jnp.bfloat16) for part in (high, middle, low))


def place(onehot, values):
    rows, lanes = values.shape
    width = -(-lanes // 128) * 128
    parts = [jnp.pad(part, ((0, 0), (0, width - lanes))) for part in split3(values)]
    out = jnp.dot(onehot, jnp.concatenate(parts, axis=1), preferred_element_type=jnp.float32)
    total = (out[:, :width] + out[:, width : 2 * width]) + out[:, 2 * width :]
    return total[:, :lanes]


def chebyshev(start, residual_now, operator_fn, inverse_diag, upper_bound, keep_last):
    low_end = upper_bound * lower_share
    center = 0.5 * (upper_bound + low_end)
    radius = 0.5 * (upper_bound - low_end)
    sigma_value = center / radius
    rho_value = 1.0 / sigma_value
    solution = start
    update = inverse_diag * residual_now / center
    for turn_index in range(3):
        solution = solution + update
        if turn_index < 2 or keep_last:
            residual_now = residual_now - operator_fn(update)
        if turn_index < 2:
            rho_next = 1.0 / (2.0 * sigma_value - rho_value)
            update = (
                rho_next * rho_value * update
                + 2.0 * rho_next / radius * inverse_diag * residual_now
            )
            rho_value = rho_next
    return (solution, residual_now)


def onehot_of(rows_ids, column_ids):
    return (rows_ids[:, None] == column_ids[None, :]).astype(jnp.bfloat16)


def level_plan(local_ids, left_ids, right_ids):
    face_count = local_ids.shape[0]
    elem_count = face_count // 6
    has_local = local_ids >= 0
    source = jnp.where(has_local, local_ids, 0)
    send_ids = jnp.concatenate([left_ids, right_ids])
    face_of = send_ids // elem_count
    block_of = jnp.arange(6 * 128, dtype=jnp.int32) // 128
    in_block = face_of[:, None] == block_of[None, :]
    onehot = onehot_of(jnp.arange(elem_count, dtype=jnp.int32), send_ids % elem_count)
    onehot = onehot.astype(jnp.float32)
    return has_local, source, send_ids, in_block, onehot


def apply_level(vector_t, scale_col, plan, mats):
    has_local, source, send_ids, in_block, onehot = plan
    stiffness_t, pick, fold, weight = mats
    elem_count = vector_t.shape[0]
    shared = send_ids.shape[0] // 2
    parts = jnp.concatenate(
        [jnp.pad(part, ((0, 0), (0, 3))) for part in split3(vector_t)], axis=1
    )
    faces = jnp.concatenate(
        [jnp.dot(parts, pick[f], preferred_element_type=jnp.float32) for f in range(6)], axis=0
    )
    from_left = passed_along(faces[send_ids[shared:]], AXES, 1)
    from_right = passed_along(faces[send_ids[:shared]], AXES, -1)
    partner = jnp.where(has_local[:, None], faces[source], 0.0)
    jump = (faces - partner).reshape(6, elem_count, 128) * weight[:, None, :]
    folded = lax.dot_general(
        jump, fold, (((0, 2), (0, 1)), ((), ())), precision=lax.Precision.HIGH
    )
    received = jnp.concatenate([from_left, from_right], axis=0)
    spread = jnp.where(in_block, jnp.tile(received, (1, 6)) * weight.reshape(1, 6 * 128), 0.0)
    shared_terms = jnp.dot(spread, fold.reshape(6 * 128, 125), precision=highest)
    interior = scale_col * jnp.dot(vector_t, stiffness_t, precision=highest)
    return (interior + folded) - jnp.dot(onehot, shared_terms, precision=highest)


def interpolate_t(values_t, code_row, mats):
    mixed = jnp.dot(values_t, mats, precision=highest)
    out = jnp.zeros_like(values_t)
    for q in range(9):
        out = jnp.where(code_row[:, None] == q, mixed[:, 128 * q : 128 * q + 125], out)
    return out


def on_device(
    load_vector,
    fine_scale,
    coarse_scale,
    parent_owner,
    parent_pos,
    child_code,
    arrival_slot,
    fine_local,
    fine_left,
    fine_right,
    coarse_local,
    coarse_left,
    coarse_right,
):
    stiffness, extract, face_weight, face_diag, stiff_diag, upper_bound, halves, face_nodes = (
        element_tables()
    )
    pick = np.zeros((6, 125, 128))
    fold = np.zeros((6, 128, 125))
    weight = np.zeros((6, 128))
    for f in range(6):
        for m in range(25):
            pick[f, face_nodes[f, m], m] = 1.0
            fold[f, m, face_nodes[f, m]] = penalty_weight
            weight[f, m] = face_weight[f, m]
    prolong = np.zeros((125, 9 * 128))
    restrict = np.zeros((125, 9 * 128))
    for q in range(9):
        if q == 8:
            matrix = np.eye(125)
        else:
            matrix = np.kron(np.kron(halves[(q // 4) % 2], halves[(q // 2) % 2]), halves[q % 2])
        prolong[:, 128 * q : 128 * q + 125] = matrix.T
        restrict[:, 128 * q : 128 * q + 125] = matrix
    f32 = lambda a: jnp.asarray(a, jnp.float32)
    pick = np.concatenate([np.pad(pick, ((0, 0), (0, 3), (0, 0)))] * 3, axis=1)
    mats = (f32(stiffness.T), jnp.asarray(pick, jnp.bfloat16), f32(fold), f32(weight))
    prolong = f32(prolong)
    restrict = f32(restrict)
    face_diag = f32(face_diag)
    stiff_diag = f32(stiff_diag)

    fine_plan = level_plan(fine_local, fine_left, fine_right)
    coarse_plan = level_plan(coarse_local, coarse_left, coarse_right)
    fine_col = fine_scale[:, None]
    coarse_col = coarse_scale[:, None]

    def fine_apply(vector_t):
        return apply_level(vector_t, fine_col, fine_plan, mats)

    def coarse_apply(vector_t):
        return apply_level(vector_t, coarse_col, coarse_plan, mats)

    def inverse_diagonal(scale_col):
        return 1.0 / (scale_col * stiff_diag[None, :] + penalty_weight * face_diag[None, :])

    fine_inverse = inverse_diagonal(fine_col)
    coarse_inverse = inverse_diagonal(coarse_col)
    load_t = load_vector.T
    first_x, first_r = chebyshev(
        jnp.zeros_like(load_t), load_t, fine_apply, fine_inverse, upper_bound, True
    )
    rank_count = lax.axis_size(AXES)
    slot_count = arrival_slot.shape[0]
    capacity = slot_count // rank_count
    coarse_count = coarse_scale.shape[0]
    target = parent_owner * capacity + parent_pos
    slot_ids = jnp.arange(slot_count, dtype=jnp.int32)
    coarse_ids = jnp.arange(coarse_count, dtype=jnp.int32)

    pieces = interpolate_t(first_r, child_code, restrict)
    buffer = place(onehot_of(slot_ids, target), pieces)
    arrived = lax.all_to_all(buffer, AXES, 0, 0, tiled=True)
    coarse_rhs = place(onehot_of(coarse_ids, arrival_slot), arrived)
    coarse_x, unused_r = chebyshev(
        jnp.zeros_like(coarse_rhs), coarse_rhs, coarse_apply, coarse_inverse, upper_bound, False
    )
    filled = place(onehot_of(arrival_slot, coarse_ids), coarse_x)
    returned = lax.all_to_all(filled, AXES, 0, 0, tiled=True)
    correction = interpolate_t(place(onehot_of(target, slot_ids), returned), child_code, prolong)
    second_x = first_x + correction
    second_r = first_r - fine_apply(correction)
    final_x, final_r = chebyshev(second_x, second_r, fine_apply, fine_inverse, upper_bound, True)
    return (final_x.T, final_r.T)


def solution(mesh):
    in_specs = (P(None, AXES),) + (P(AXES),) * 12
    out_specs = (P(None, AXES), P(None, AXES))
    return jax.shard_map(
        on_device, mesh=mesh, in_specs=in_specs, out_specs=out_specs, check_vma=False
    )
```

```python
import math

import jax
import jax.numpy as jnp
import numpy as np
from jax import lax
from jax.sharding import PartitionSpec as P

highest = lax.Precision.HIGHEST
penalty_weight = 20.0
lower_share = 0.125
AXES = ("elem", "sub")


def passed_along(block, axis, distance):
    devices = range(lax.axis_size(axis))
    route = [(i - distance, i) for i in devices if i - distance in devices]
    return lax.ppermute(block, axis, route)


def lagrange_rows(points, gll_points):
    values = np.ones((points.shape[0], 5))
    for column in range(5):
        for other_node in range(5):
            if other_node != column:
                values[:, column] *= (points - gll_points[other_node]) / (
                    gll_points[column] - gll_points[other_node]
                )
    return values


def element_tables():
    root_value = math.sqrt(3.0 / 7.0)
    gll_points = np.array([-1.0, -root_value, 0.0, root_value, 1.0])
    gll_weights = np.array([0.1, 49.0 / 90.0, 32.0 / 45.0, 49.0 / 90.0, 0.1])
    identity_mask = np.arange(5)[:, None] == np.arange(5)[None, :]
    spread = gll_points[:, None] - gll_points[None, :]
    spread = np.where(identity_mask, 1.0, spread)
    factor = np.prod(spread, axis=1)
    derive = factor[:, None] / factor[None, :] / spread
    diag_values = np.sum(1.0 / spread, axis=1) - 1.0
    derive = np.where(identity_mask, diag_values[:, None], derive)
    stiff_line = derive.T @ (gll_weights[:, None] * derive)
    mass_line = np.where(identity_mask, gll_weights[None, :], 0.0)
    stiffness = (
        np.kron(np.kron(stiff_line, mass_line), mass_line)
        + np.kron(np.kron(mass_line, stiff_line), mass_line)
        + np.kron(np.kron(mass_line, mass_line), stiff_line)
    )
    extract = np.zeros((150, 125))
    face_weight = np.zeros((6, 25))
    face_nodes = np.zeros((6, 25), np.int64)
    for normal in range(3):
        for side_pick in range(2):
            face_id = 2 * normal + side_pick
            for first_pos in range(5):
                for second_pos in range(5):
                    triple = [first_pos, second_pos]
                    triple.insert(normal, 4 * side_pick)
                    node_id = 25 * triple[0] + 5 * triple[1] + triple[2]
                    extract[25 * face_id + 5 * first_pos + second_pos, node_id] = 1.0
                    face_nodes[face_id, 5 * first_pos + second_pos] = node_id
                    face_weight[face_id, 5 * first_pos + second_pos] = (
                        gll_weights[first_pos] * gll_weights[second_pos]
                    )
    face_diag = extract.T @ face_weight.reshape(150)
    node_range = np.arange(125)
    stiff_diag = stiffness[node_range, node_range].copy()
    upper_bound = max(2.0, float(np.max(np.sum(np.abs(stiffness), axis=1) / stiff_diag)))
    halves = np.stack(
        [
            lagrange_rows((gll_points - 1.0) / 2.0, gll_points),
            lagrange_rows((gll_points + 1.0) / 2.0, gll_points),
        ]
    )
    return (stiffness, extract, face_weight, face_diag, stiff_diag, upper_bound, halves, face_nodes)


def to_bf16_grid(values):
    return lax.reduce_precision(values, exponent_bits=8, mantissa_bits=7)


def split3(values):
    high = to_bf16_grid(values)
    rest = values - high
    middle = to_bf16_grid(rest)
    low = rest - middle
    return tuple(part.astype(jnp.bfloat16) for part in (high, middle, low))


def place(onehot, values):
    rows, lanes = values.shape
    width = -(-lanes // 128) * 128
    parts = [jnp.pad(part, ((0, 0), (0, width - lanes))) for part in split3(values)]
    out = jnp.dot(onehot, jnp.concatenate(parts, axis=1), preferred_element_type=jnp.float32)
    total = (out[:, :width] + out[:, width : 2 * width]) + out[:, 2 * width :]
    return total[:, :lanes]


def chebyshev(start, residual_now, operator_fn, inverse_diag, upper_bound, keep_last):
    low_end = upper_bound * lower_share
    center = 0.5 * (upper_bound + low_end)
    radius = 0.5 * (upper_bound - low_end)
    sigma_value = center / radius
    rho_value = 1.0 / sigma_value
    solution = start
    update = inverse_diag * residual_now / center
    for turn_index in range(3):
        solution = solution + update
        if turn_index < 2 or keep_last:
            residual_now = residual_now - operator_fn(update)
        if turn_index < 2:
            rho_next = 1.0 / (2.0 * sigma_value - rho_value)
            update = (
                rho_next * rho_value * update
                + 2.0 * rho_next / radius * inverse_diag * residual_now
            )
            rho_value = rho_next
    return (solution, residual_now)


def onehot_of(rows_ids, column_ids):
    return (rows_ids[:, None] == column_ids[None, :]).astype(jnp.bfloat16)


def level_plan(local_ids, left_ids, right_ids):
    face_count = local_ids.shape[0]
    elem_count = face_count // 6
    has_local = local_ids >= 0
    source = jnp.where(has_local, local_ids, 0)
    send_ids = jnp.concatenate([left_ids, right_ids])
    face_of = send_ids // elem_count
    block_of = jnp.arange(6 * 128, dtype=jnp.int32) // 128
    in_block = face_of[:, None] == block_of[None, :]
    onehot = onehot_of(jnp.arange(elem_count, dtype=jnp.int32), send_ids % elem_count)
    onehot = onehot.astype(jnp.float32)
    return has_local, source, send_ids, in_block, onehot


def apply_level(vector_t, scale_col, plan, mats):
    has_local, source, send_ids, in_block, onehot = plan
    stiffness_t, pick, fold, weight = mats
    elem_count = vector_t.shape[0]
    shared = send_ids.shape[0] // 2
    faces = jnp.concatenate(
        [jnp.dot(vector_t, pick[f], precision=highest) for f in range(6)], axis=0
    )
    from_left = passed_along(faces[send_ids[shared:]], AXES, 1)
    from_right = passed_along(faces[send_ids[:shared]], AXES, -1)
    partner = jnp.where(has_local[:, None], faces[source], 0.0)
    jump = (faces - partner).reshape(6, elem_count, 128) * weight[:, None, :]
    folded = lax.dot_general(
        jump, fold, (((0, 2), (0, 1)), ((), ())), precision=lax.Precision.HIGH
    )
    received = jnp.concatenate([from_left, from_right], axis=0)
    spread = jnp.where(in_block, jnp.tile(received, (1, 6)) * weight.reshape(1, 6 * 128), 0.0)
    shared_terms = jnp.dot(spread, fold.reshape(6 * 128, 125), precision=highest)
    interior = scale_col * jnp.dot(vector_t, stiffness_t, precision=highest)
    return (interior + folded) - jnp.dot(onehot, shared_terms, precision=highest)


def interpolate_t(values_t, code_row, mats):
    mixed = jnp.dot(values_t, mats, precision=lax.Precision.HIGH)
    out = jnp.zeros_like(values_t)
    for q in range(9):
        out = jnp.where(code_row[:, None] == q, mixed[:, 128 * q : 128 * q + 125], out)
    return out


def on_device(
    load_vector,
    fine_scale,
    coarse_scale,
    parent_owner,
    parent_pos,
    child_code,
    arrival_slot,
    fine_local,
    fine_left,
    fine_right,
    coarse_local,
    coarse_left,
    coarse_right,
):
    stiffness, extract, face_weight, face_diag, stiff_diag, upper_bound, halves, face_nodes = (
        element_tables()
    )
    pick = np.zeros((6, 125, 128))
    fold = np.zeros((6, 128, 125))
    weight = np.zeros((6, 128))
    for f in range(6):
        for m in range(25):
            pick[f, face_nodes[f, m], m] = 1.0
            fold[f, m, face_nodes[f, m]] = penalty_weight
            weight[f, m] = face_weight[f, m]
    prolong = np.zeros((125, 9 * 128))
    restrict = np.zeros((125, 9 * 128))
    for q in range(9):
        if q == 8:
            matrix = np.eye(125)
        else:
            matrix = np.kron(np.kron(halves[(q // 4) % 2], halves[(q // 2) % 2]), halves[q % 2])
        prolong[:, 128 * q : 128 * q + 125] = matrix.T
        restrict[:, 128 * q : 128 * q + 125] = matrix
    f32 = lambda a: jnp.asarray(a, jnp.float32)
    mats = (f32(stiffness.T), f32(pick), f32(fold), f32(weight))
    prolong = f32(prolong)
    restrict = f32(restrict)
    face_diag = f32(face_diag)
    stiff_diag = f32(stiff_diag)

    fine_plan = level_plan(fine_local, fine_left, fine_right)
    coarse_plan = level_plan(coarse_local, coarse_left, coarse_right)
    fine_col = fine_scale[:, None]
    coarse_col = coarse_scale[:, None]

    def fine_apply(vector_t):
        return apply_level(vector_t, fine_col, fine_plan, mats)

    def coarse_apply(vector_t):
        return apply_level(vector_t, coarse_col, coarse_plan, mats)

    def inverse_diagonal(scale_col):
        return 1.0 / (scale_col * stiff_diag[None, :] + penalty_weight * face_diag[None, :])

    fine_inverse = inverse_diagonal(fine_col)
    coarse_inverse = inverse_diagonal(coarse_col)
    load_t = load_vector.T
    first_x, first_r = chebyshev(
        jnp.zeros_like(load_t), load_t, fine_apply, fine_inverse, upper_bound, True
    )
    rank_count = lax.axis_size(AXES)
    slot_count = arrival_slot.shape[0]
    capacity = slot_count // rank_count
    coarse_count = coarse_scale.shape[0]
    target = parent_owner * capacity + parent_pos
    slot_ids = jnp.arange(slot_count, dtype=jnp.int32)
    coarse_ids = jnp.arange(coarse_count, dtype=jnp.int32)

    pieces = interpolate_t(first_r, child_code, restrict)
    buffer = place(onehot_of(slot_ids, target), pieces)
    arrived = lax.all_to_all(buffer, AXES, 0, 0, tiled=True)
    coarse_rhs = place(onehot_of(coarse_ids, arrival_slot), arrived)
    coarse_x, unused_r = chebyshev(
        jnp.zeros_like(coarse_rhs), coarse_rhs, coarse_apply, coarse_inverse, upper_bound, False
    )
    filled = place(onehot_of(arrival_slot, coarse_ids), coarse_x)
    returned = lax.all_to_all(filled, AXES, 0, 0, tiled=True)
    correction = interpolate_t(place(onehot_of(target, slot_ids), returned), child_code, prolong)
    second_x = first_x + correction
    second_r = first_r - fine_apply(correction)
    final_x, final_r = chebyshev(second_x, second_r, fine_apply, fine_inverse, upper_bound, True)
    return (final_x.T, final_r.T)


def solution(mesh):
    in_specs = (P(None, AXES),) + (P(AXES),) * 12
    out_specs = (P(None, AXES), P(None, AXES))
    return jax.shard_map(
        on_device, mesh=mesh, in_specs=in_specs, out_specs=out_specs, check_vma=False
    )
```

```python
import math

import jax
import jax.numpy as jnp
import numpy as np
from jax import lax
from jax.sharding import PartitionSpec as P

highest = lax.Precision.HIGHEST
penalty_weight = 20.0
lower_share = 0.125
AXES = ("elem", "sub")


def passed_along(block, axis, distance):
    devices = range(lax.axis_size(axis))
    route = [(i - distance, i) for i in devices if i - distance in devices]
    return lax.ppermute(block, axis, route)


def lagrange_rows(points, gll_points):
    values = np.ones((points.shape[0], 5))
    for column in range(5):
        for other_node in range(5):
            if other_node != column:
                values[:, column] *= (points - gll_points[other_node]) / (
                    gll_points[column] - gll_points[other_node]
                )
    return values


def element_tables():
    root_value = math.sqrt(3.0 / 7.0)
    gll_points = np.array([-1.0, -root_value, 0.0, root_value, 1.0])
    gll_weights = np.array([0.1, 49.0 / 90.0, 32.0 / 45.0, 49.0 / 90.0, 0.1])
    identity_mask = np.arange(5)[:, None] == np.arange(5)[None, :]
    spread = gll_points[:, None] - gll_points[None, :]
    spread = np.where(identity_mask, 1.0, spread)
    factor = np.prod(spread, axis=1)
    derive = factor[:, None] / factor[None, :] / spread
    diag_values = np.sum(1.0 / spread, axis=1) - 1.0
    derive = np.where(identity_mask, diag_values[:, None], derive)
    stiff_line = derive.T @ (gll_weights[:, None] * derive)
    mass_line = np.where(identity_mask, gll_weights[None, :], 0.0)
    stiffness = (
        np.kron(np.kron(stiff_line, mass_line), mass_line)
        + np.kron(np.kron(mass_line, stiff_line), mass_line)
        + np.kron(np.kron(mass_line, mass_line), stiff_line)
    )
    extract = np.zeros((150, 125))
    face_weight = np.zeros((6, 25))
    face_nodes = np.zeros((6, 25), np.int64)
    for normal in range(3):
        for side_pick in range(2):
            face_id = 2 * normal + side_pick
            for first_pos in range(5):
                for second_pos in range(5):
                    triple = [first_pos, second_pos]
                    triple.insert(normal, 4 * side_pick)
                    node_id = 25 * triple[0] + 5 * triple[1] + triple[2]
                    extract[25 * face_id + 5 * first_pos + second_pos, node_id] = 1.0
                    face_nodes[face_id, 5 * first_pos + second_pos] = node_id
                    face_weight[face_id, 5 * first_pos + second_pos] = (
                        gll_weights[first_pos] * gll_weights[second_pos]
                    )
    face_diag = extract.T @ face_weight.reshape(150)
    node_range = np.arange(125)
    stiff_diag = stiffness[node_range, node_range].copy()
    upper_bound = max(2.0, float(np.max(np.sum(np.abs(stiffness), axis=1) / stiff_diag)))
    halves = np.stack(
        [
            lagrange_rows((gll_points - 1.0) / 2.0, gll_points),
            lagrange_rows((gll_points + 1.0) / 2.0, gll_points),
        ]
    )
    return (stiffness, extract, face_weight, face_diag, stiff_diag, upper_bound, halves, face_nodes)


def to_bf16_grid(values):
    return lax.reduce_precision(values, exponent_bits=8, mantissa_bits=7)


def split3(values):
    high = to_bf16_grid(values)
    rest = values - high
    middle = to_bf16_grid(rest)
    low = rest - middle
    return tuple(part.astype(jnp.bfloat16) for part in (high, middle, low))


def place(onehot, values):
    rows, lanes = values.shape
    width = -(-lanes // 128) * 128
    parts = [jnp.pad(part, ((0, 0), (0, width - lanes))) for part in split3(values)]
    out = jnp.dot(onehot, jnp.concatenate(parts, axis=1), preferred_element_type=jnp.float32)
    total = (out[:, :width] + out[:, width : 2 * width]) + out[:, 2 * width :]
    return total[:, :lanes]


def chebyshev(start, residual_now, operator_fn, inverse_diag, upper_bound, keep_last):
    low_end = upper_bound * lower_share
    center = 0.5 * (upper_bound + low_end)
    radius = 0.5 * (upper_bound - low_end)
    sigma_value = center / radius
    rho_value = 1.0 / sigma_value
    solution = start
    update = inverse_diag * residual_now / center
    for turn_index in range(3):
        solution = solution + update
        if turn_index < 2 or keep_last:
            residual_now = residual_now - operator_fn(update)
        if turn_index < 2:
            rho_next = 1.0 / (2.0 * sigma_value - rho_value)
            update = (
                rho_next * rho_value * update
                + 2.0 * rho_next / radius * inverse_diag * residual_now
            )
            rho_value = rho_next
    return (solution, residual_now)


def onehot_of(rows_ids, column_ids):
    return (rows_ids[:, None] == column_ids[None, :]).astype(jnp.bfloat16)


def level_plan(local_ids, left_ids, right_ids):
    face_count = local_ids.shape[0]
    elem_count = face_count // 6
    has_local = local_ids >= 0
    source = jnp.where(has_local, local_ids, 0)
    send_ids = jnp.concatenate([left_ids, right_ids])
    face_of = send_ids // elem_count
    block_of = jnp.arange(6 * 128, dtype=jnp.int32) // 128
    in_block = face_of[:, None] == block_of[None, :]
    onehot = onehot_of(jnp.arange(elem_count, dtype=jnp.int32), send_ids % elem_count)
    onehot = onehot.astype(jnp.float32)
    plan = (has_local, source.astype(jnp.uint32), send_ids.astype(jnp.uint32), in_block, onehot)
    return lax.optimization_barrier(plan)


def apply_level(vector_t, scale_col, plan, mats):
    has_local, source, send_ids, in_block, onehot = plan
    stiffness_t, pick, fold, weight = mats
    elem_count = vector_t.shape[0]
    shared = send_ids.shape[0] // 2
    faces = jnp.concatenate(
        [jnp.dot(vector_t, pick[f], precision=highest) for f in range(6)], axis=0
    )
    from_left = passed_along(faces[send_ids[shared:]], AXES, 1)
    from_right = passed_along(faces[send_ids[:shared]], AXES, -1)
    partner = jnp.where(has_local[:, None], faces[source], 0.0)
    jump = (faces - partner).reshape(6, elem_count, 128) * weight[:, None, :]
    folded = lax.dot_general(
        jump, fold, (((0, 2), (0, 1)), ((), ())), precision=lax.Precision.HIGH
    )
    received = jnp.concatenate([from_left, from_right], axis=0)
    spread = jnp.where(in_block, jnp.tile(received, (1, 6)) * weight.reshape(1, 6 * 128), 0.0)
    shared_terms = jnp.dot(spread, fold.reshape(6 * 128, 125), precision=highest)
    interior = scale_col * jnp.dot(vector_t, stiffness_t, precision=highest)
    return (interior + folded) - jnp.dot(onehot, shared_terms, precision=highest)


def interpolate_t(values_t, code_row, mats):
    mixed = jnp.dot(values_t, mats, precision=lax.Precision.HIGH)
    out = jnp.zeros_like(values_t)
    for q in range(9):
        out = jnp.where(code_row[:, None] == q, mixed[:, 128 * q : 128 * q + 125], out)
    return out


def on_device(
    load_vector,
    fine_scale,
    coarse_scale,
    parent_owner,
    parent_pos,
    child_code,
    arrival_slot,
    fine_local,
    fine_left,
    fine_right,
    coarse_local,
    coarse_left,
    coarse_right,
):
    stiffness, extract, face_weight, face_diag, stiff_diag, upper_bound, halves, face_nodes = (
        element_tables()
    )
    pick = np.zeros((6, 125, 128))
    fold = np.zeros((6, 128, 125))
    weight = np.zeros((6, 128))
    for f in range(6):
        for m in range(25):
            pick[f, face_nodes[f, m], m] = 1.0
            fold[f, m, face_nodes[f, m]] = penalty_weight
            weight[f, m] = face_weight[f, m]
    prolong = np.zeros((125, 9 * 128))
    restrict = np.zeros((125, 9 * 128))
    for q in range(9):
        if q == 8:
            matrix = np.eye(125)
        else:
            matrix = np.kron(np.kron(halves[(q // 4) % 2], halves[(q // 2) % 2]), halves[q % 2])
        prolong[:, 128 * q : 128 * q + 125] = matrix.T
        restrict[:, 128 * q : 128 * q + 125] = matrix
    f32 = lambda a: jnp.asarray(a, jnp.float32)
    mats = (f32(stiffness.T), f32(pick), f32(fold), f32(weight))
    prolong = f32(prolong)
    restrict = f32(restrict)
    face_diag = f32(face_diag)
    stiff_diag = f32(stiff_diag)

    fine_plan = level_plan(fine_local, fine_left, fine_right)
    coarse_plan = level_plan(coarse_local, coarse_left, coarse_right)
    fine_col = fine_scale[:, None]
    coarse_col = coarse_scale[:, None]

    def fine_apply(vector_t):
        return apply_level(vector_t, fine_col, fine_plan, mats)

    def coarse_apply(vector_t):
        return apply_level(vector_t, coarse_col, coarse_plan, mats)

    def inverse_diagonal(scale_col):
        return 1.0 / (scale_col * stiff_diag[None, :] + penalty_weight * face_diag[None, :])

    fine_inverse = inverse_diagonal(fine_col)
    coarse_inverse = inverse_diagonal(coarse_col)
    load_t = load_vector.T
    first_x, first_r = chebyshev(
        jnp.zeros_like(load_t), load_t, fine_apply, fine_inverse, upper_bound, True
    )
    rank_count = lax.axis_size(AXES)
    slot_count = arrival_slot.shape[0]
    capacity = slot_count // rank_count
    coarse_count = coarse_scale.shape[0]
    target = parent_owner * capacity + parent_pos
    slot_ids = jnp.arange(slot_count, dtype=jnp.int32)
    coarse_ids = jnp.arange(coarse_count, dtype=jnp.int32)

    pieces = interpolate_t(first_r, child_code, restrict)
    buffer = place(onehot_of(slot_ids, target), pieces)
    arrived = lax.all_to_all(buffer, AXES, 0, 0, tiled=True)
    coarse_rhs = place(onehot_of(coarse_ids, arrival_slot), arrived)
    coarse_x, unused_r = chebyshev(
        jnp.zeros_like(coarse_rhs), coarse_rhs, coarse_apply, coarse_inverse, upper_bound, False
    )
    filled = place(onehot_of(arrival_slot, coarse_ids), coarse_x)
    returned = lax.all_to_all(filled, AXES, 0, 0, tiled=True)
    correction = interpolate_t(place(onehot_of(target, slot_ids), returned), child_code, prolong)
    second_x = first_x + correction
    second_r = first_r - fine_apply(correction)
    final_x, final_r = chebyshev(second_x, second_r, fine_apply, fine_inverse, upper_bound, True)
    return (final_x.T, final_r.T)


def solution(mesh):
    in_specs = (P(None, AXES),) + (P(AXES),) * 12
    out_specs = (P(None, AXES), P(None, AXES))
    return jax.shard_map(
        on_device, mesh=mesh, in_specs=in_specs, out_specs=out_specs, check_vma=False
    )
```

```python
import math

import jax
import jax.numpy as jnp
import numpy as np
from jax import lax
from jax.sharding import PartitionSpec as P

highest = lax.Precision.HIGHEST
penalty_weight = 20.0
lower_share = 0.125
AXES = ("elem", "sub")


def passed_along(block, axis, distance):
    devices = range(lax.axis_size(axis))
    route = [(i - distance, i) for i in devices if i - distance in devices]
    return lax.ppermute(block, axis, route)


def lagrange_rows(points, gll_points):
    values = np.ones((points.shape[0], 5))
    for column in range(5):
        for other_node in range(5):
            if other_node != column:
                values[:, column] *= (points - gll_points[other_node]) / (
                    gll_points[column] - gll_points[other_node]
                )
    return values


def element_tables():
    root_value = math.sqrt(3.0 / 7.0)
    gll_points = np.array([-1.0, -root_value, 0.0, root_value, 1.0])
    gll_weights = np.array([0.1, 49.0 / 90.0, 32.0 / 45.0, 49.0 / 90.0, 0.1])
    identity_mask = np.arange(5)[:, None] == np.arange(5)[None, :]
    spread = gll_points[:, None] - gll_points[None, :]
    spread = np.where(identity_mask, 1.0, spread)
    factor = np.prod(spread, axis=1)
    derive = factor[:, None] / factor[None, :] / spread
    diag_values = np.sum(1.0 / spread, axis=1) - 1.0
    derive = np.where(identity_mask, diag_values[:, None], derive)
    stiff_line = derive.T @ (gll_weights[:, None] * derive)
    mass_line = np.where(identity_mask, gll_weights[None, :], 0.0)
    stiffness = (
        np.kron(np.kron(stiff_line, mass_line), mass_line)
        + np.kron(np.kron(mass_line, stiff_line), mass_line)
        + np.kron(np.kron(mass_line, mass_line), stiff_line)
    )
    extract = np.zeros((150, 125))
    face_weight = np.zeros((6, 25))
    face_nodes = np.zeros((6, 25), np.int64)
    for normal in range(3):
        for side_pick in range(2):
            face_id = 2 * normal + side_pick
            for first_pos in range(5):
                for second_pos in range(5):
                    triple = [first_pos, second_pos]
                    triple.insert(normal, 4 * side_pick)
                    node_id = 25 * triple[0] + 5 * triple[1] + triple[2]
                    extract[25 * face_id + 5 * first_pos + second_pos, node_id] = 1.0
                    face_nodes[face_id, 5 * first_pos + second_pos] = node_id
                    face_weight[face_id, 5 * first_pos + second_pos] = (
                        gll_weights[first_pos] * gll_weights[second_pos]
                    )
    face_diag = extract.T @ face_weight.reshape(150)
    node_range = np.arange(125)
    stiff_diag = stiffness[node_range, node_range].copy()
    upper_bound = max(2.0, float(np.max(np.sum(np.abs(stiffness), axis=1) / stiff_diag)))
    halves = np.stack(
        [
            lagrange_rows((gll_points - 1.0) / 2.0, gll_points),
            lagrange_rows((gll_points + 1.0) / 2.0, gll_points),
        ]
    )
    return (stiffness, extract, face_weight, face_diag, stiff_diag, upper_bound, halves, face_nodes)


def to_bf16_grid(values):
    return lax.reduce_precision(values, exponent_bits=8, mantissa_bits=7)


def split3(values):
    high = to_bf16_grid(values)
    rest = values - high
    middle = to_bf16_grid(rest)
    low = rest - middle
    return tuple(part.astype(jnp.bfloat16) for part in (high, middle, low))


def place(onehot, values):
    rows, lanes = values.shape
    width = -(-lanes // 128) * 128
    parts = [jnp.pad(part, ((0, 0), (0, width - lanes))) for part in split3(values)]
    out = jnp.dot(onehot, jnp.concatenate(parts, axis=1), preferred_element_type=jnp.float32)
    total = (out[:, :width] + out[:, width : 2 * width]) + out[:, 2 * width :]
    return total[:, :lanes]


def chebyshev(start, residual_now, operator_fn, inverse_diag, upper_bound, keep_last):
    low_end = upper_bound * lower_share
    center = 0.5 * (upper_bound + low_end)
    radius = 0.5 * (upper_bound - low_end)
    sigma_value = center / radius
    rho_value = 1.0 / sigma_value
    solution = start
    update = inverse_diag * residual_now / center
    for turn_index in range(3):
        solution = solution + update
        if turn_index < 2 or keep_last:
            residual_now = residual_now - operator_fn(update)
        if turn_index < 2:
            rho_next = 1.0 / (2.0 * sigma_value - rho_value)
            update = (
                rho_next * rho_value * update
                + 2.0 * rho_next / radius * inverse_diag * residual_now
            )
            rho_value = rho_next
    return (solution, residual_now)


def onehot_of(rows_ids, column_ids):
    return (rows_ids[:, None] == column_ids[None, :]).astype(jnp.bfloat16)


def level_plan(local_ids, left_ids, right_ids):
    face_count = local_ids.shape[0]
    elem_count = face_count // 6
    has_local = local_ids >= 0
    source = jnp.where(has_local, local_ids, 0)
    send_ids = jnp.concatenate([left_ids, right_ids])
    face_of = send_ids // elem_count
    block_of = jnp.arange(6 * 128, dtype=jnp.int32) // 128
    in_block = face_of[:, None] == block_of[None, :]
    onehot = onehot_of(jnp.arange(elem_count, dtype=jnp.int32), send_ids % elem_count)
    onehot = onehot.astype(jnp.float32)
    return has_local, source, send_ids, in_block, onehot


def apply_level(vector_t, scale_col, plan, mats):
    has_local, source, send_ids, in_block, onehot = plan
    stiffness_t, pick, fold, weight = mats
    elem_count = vector_t.shape[0]
    shared = send_ids.shape[0] // 2
    faces = jnp.concatenate(
        [jnp.dot(vector_t, pick[f], precision=highest) for f in range(6)], axis=0
    )
    from_left = passed_along(faces[send_ids[shared:]], AXES, 1)
    from_right = passed_along(faces[send_ids[:shared]], AXES, -1)
    partner = jnp.where(has_local[:, None], faces[source], 0.0)
    jump = (faces - partner).reshape(6, elem_count, 128) * weight[:, None, :]
    folded = lax.dot_general(
        jump, fold, (((0, 2), (0, 1)), ((), ())), precision=lax.Precision.HIGH
    )
    received = jnp.concatenate([from_left, from_right], axis=0)
    spread = jnp.where(in_block, jnp.tile(received, (1, 6)) * weight.reshape(1, 6 * 128), 0.0)
    shared_terms = jnp.dot(spread, fold.reshape(6 * 128, 125), precision=lax.Precision.HIGH)
    interior = scale_col * jnp.dot(vector_t, stiffness_t, precision=highest)
    return (interior + folded) - jnp.dot(onehot, shared_terms, precision=lax.Precision.HIGH)


def interpolate_t(values_t, code_row, mats):
    mixed = jnp.dot(values_t, mats, precision=lax.Precision.HIGH)
    out = jnp.zeros_like(values_t)
    for q in range(9):
        out = jnp.where(code_row[:, None] == q, mixed[:, 128 * q : 128 * q + 125], out)
    return out


def on_device(
    load_vector,
    fine_scale,
    coarse_scale,
    parent_owner,
    parent_pos,
    child_code,
    arrival_slot,
    fine_local,
    fine_left,
    fine_right,
    coarse_local,
    coarse_left,
    coarse_right,
):
    stiffness, extract, face_weight, face_diag, stiff_diag, upper_bound, halves, face_nodes = (
        element_tables()
    )
    pick = np.zeros((6, 125, 128))
    fold = np.zeros((6, 128, 125))
    weight = np.zeros((6, 128))
    for f in range(6):
        for m in range(25):
            pick[f, face_nodes[f, m], m] = 1.0
            fold[f, m, face_nodes[f, m]] = penalty_weight
            weight[f, m] = face_weight[f, m]
    prolong = np.zeros((125, 9 * 128))
    restrict = np.zeros((125, 9 * 128))
    for q in range(9):
        if q == 8:
            matrix = np.eye(125)
        else:
            matrix = np.kron(np.kron(halves[(q // 4) % 2], halves[(q // 2) % 2]), halves[q % 2])
        prolong[:, 128 * q : 128 * q + 125] = matrix.T
        restrict[:, 128 * q : 128 * q + 125] = matrix
    f32 = lambda a: jnp.asarray(a, jnp.float32)
    mats = (f32(stiffness.T), f32(pick), f32(fold), f32(weight))
    prolong = f32(prolong)
    restrict = f32(restrict)
    face_diag = f32(face_diag)
    stiff_diag = f32(stiff_diag)

    fine_plan = level_plan(fine_local, fine_left, fine_right)
    coarse_plan = level_plan(coarse_local, coarse_left, coarse_right)
    fine_col = fine_scale[:, None]
    coarse_col = coarse_scale[:, None]

    def fine_apply(vector_t):
        return apply_level(vector_t, fine_col, fine_plan, mats)

    def coarse_apply(vector_t):
        return apply_level(vector_t, coarse_col, coarse_plan, mats)

    def inverse_diagonal(scale_col):
        return 1.0 / (scale_col * stiff_diag[None, :] + penalty_weight * face_diag[None, :])

    fine_inverse = inverse_diagonal(fine_col)
    coarse_inverse = inverse_diagonal(coarse_col)
    load_t = load_vector.T
    first_x, first_r = chebyshev(
        jnp.zeros_like(load_t), load_t, fine_apply, fine_inverse, upper_bound, True
    )
    rank_count = lax.axis_size(AXES)
    slot_count = arrival_slot.shape[0]
    capacity = slot_count // rank_count
    coarse_count = coarse_scale.shape[0]
    target = parent_owner * capacity + parent_pos
    slot_ids = jnp.arange(slot_count, dtype=jnp.int32)
    coarse_ids = jnp.arange(coarse_count, dtype=jnp.int32)

    pieces = interpolate_t(first_r, child_code, restrict)
    buffer = place(onehot_of(slot_ids, target), pieces)
    arrived = lax.all_to_all(buffer, AXES, 0, 0, tiled=True)
    coarse_rhs = place(onehot_of(coarse_ids, arrival_slot), arrived)
    coarse_x, unused_r = chebyshev(
        jnp.zeros_like(coarse_rhs), coarse_rhs, coarse_apply, coarse_inverse, upper_bound, False
    )
    filled = place(onehot_of(arrival_slot, coarse_ids), coarse_x)
    returned = lax.all_to_all(filled, AXES, 0, 0, tiled=True)
    correction = interpolate_t(place(onehot_of(target, slot_ids), returned), child_code, prolong)
    second_x = first_x + correction
    second_r = first_r - fine_apply(correction)
    final_x, final_r = chebyshev(second_x, second_r, fine_apply, fine_inverse, upper_bound, True)
    return (final_x.T, final_r.T)


def solution(mesh):
    in_specs = (P(None, AXES),) + (P(AXES),) * 12
    out_specs = (P(None, AXES), P(None, AXES))
    return jax.shard_map(
        on_device, mesh=mesh, in_specs=in_specs, out_specs=out_specs, check_vma=False
    )
```
